32 devices in a mesh: dp: 4 (over y, core), tile: 8 (over z, x).
Axes of the slice: x: 2, y: 2, z: 4, core: 2. Of those that a mesh axis runs over, the one named last changes fastest.
Arguments:
- queries: bfloat16 [4, 8, 1024, 1664], P('dp', 'tile'), may hold values from -48 to 48
- keys: bfloat16 [4, 8, 1024, 1664], P('dp', 'tile'), may hold values from -48 to 48
- values: bfloat16 [4, 8, 1024, 1664], P('dp', 'tile'), may hold values from -6 to 6
- page_info: int32 [4, 5], replicated, may hold values from 0 to 256, as said below
Outputs:
- llm_rows: bfloat16 [9216, 6656], P(('dp', 'tile'))
The draws below stay inside these ranges and needn't reach their ends.
Inputs may be any that keep to these rules, and one draw needn't show every extreme that they name: `page_info`: columns are 1 to 4, columns times rows is at most 7, tiles fill slots from the first tile slot on within the page, the thumbnail slot lies outside them, text rows at most 256; some page has 7 tiles starting at slot 0, some page 8 - 1 tiles ending at slot 7, and some page 256 text rows.
All inputs are finite; a program needn't handle non-finite values.
Results may differ from the reference program's by a relative error of at most 0.0047.
Values may be sent and summed in bfloat16 or wider, within the bound.
No kernel may reach another device: no remote copies, remote signals or barrier semaphores. Data moves between devices by JAX's collectives and lax.ppermute only.
A program may use at most 256 MiB of HBM per device.

```python
import jax
import jax.numpy as jnp
from jax import lax

HEADS = 13
HD = 128
GRID = 32
TXTMAX = 256
HH = 1664
TOK = 1024
SHUF = 256
PAGES = 4
SLOTS = 8
LLM_ROWS = 288


def query_key_pair(key):
    shape = (PAGES, SLOTS, TOK, HH)
    key_base = jax.random.normal(jax.random.fold_in(key, 11), shape, jnp.float32)
    query_base = jax.random.normal(jax.random.fold_in(key, 12), shape, jnp.float32)
    keys_out = key_base
    queries_out = query_base
    return (jnp.clip(queries_out, -48.0, 48.0), jnp.clip(keys_out, -48.0, 48.0))


def draw_queries(key, part):
    return query_key_pair(key)[0].astype(jnp.bfloat16)


def draw_keys(key, part):
    return query_key_pair(key)[1].astype(jnp.bfloat16)


def draw_page_info(key, part):
    width_key, rows_key, thumb_key, text_key, first_key = jax.random.split(key, 5)
    columns = jax.random.randint(width_key, (PAGES,), 1, 5)
    most_rows = (SLOTS - 1) // columns
    grid_rows = jax.random.randint(rows_key, (PAGES,), 1, most_rows + 1)
    page_ids = jnp.arange(PAGES)
    leading = page_ids == 0
    second = page_ids == 1
    pinned = leading | second
    columns = jnp.where(pinned, 1, columns)
    grid_rows = jnp.where(pinned, SLOTS - 1, grid_rows)
    tile_totals = columns * grid_rows
    firsts = jax.random.randint(first_key, (PAGES,), 0, SLOTS - tile_totals + 1)
    firsts = jnp.where(leading, 1, jnp.where(second, 0, firsts))
    picks = jax.random.randint(thumb_key, (PAGES,), 0, SLOTS - tile_totals)
    thumbs = jnp.where(picks < firsts, picks, picks + tile_totals)
    texts = jax.random.randint(text_key, (PAGES,), 0, TXTMAX + 1)
    texts = jnp.where(leading, TXTMAX, texts)
    return jnp.stack([columns, grid_rows, thumbs, texts, firsts], axis=1).astype(jnp.int32)


def block_scale(own_key, shape, cuts, smallest, high):
    gain = 1.0
    for axis_at, blocks in cuts:
        heights = jax.random.uniform(jax.random.fold_in(jax.random.fold_in(own_key, 6), axis_at), (blocks,), jnp.float32, smallest / len(cuts), high / len(cuts))
        gain = gain * jnp.repeat(jnp.exp(heights), shape[axis_at] // blocks).reshape((-1,) + (1,) * (len(shape) - 1 - axis_at))
    return gain


def gaussian(stream_key, shape, width, reach, pieces=(), held_as=jnp.bfloat16):
    drawn = width * jax.random.normal(stream_key, shape, jnp.float32)
    if pieces:
        drawn = drawn * block_scale(stream_key, shape, pieces, -0.22, 0.18)
    return jnp.clip(drawn, -reach, reach).astype(held_as)


def setup_inputs(seed: int = 0) -> dict:
    key_list = jax.random.split(jax.random.key(seed), 5)
    return {
        "queries": draw_queries(jax.random.fold_in(key_list[4], 71), 0),
        "keys": draw_keys(jax.random.fold_in(key_list[4], 71), 0),
        "values": gaussian(key_list[2], (PAGES, SLOTS, TOK, HH), 1.0, 6.0, ((0, 4), (1, 8))),
        "page_info": draw_page_info(jax.random.fold_in(key_list[4], 71), 0),
    }


NEG_FILL = -1.0e30


def block_terms(query_tile, key_tile, value_tile):
    query_heads = query_tile.reshape(TOK, HEADS, HD).astype(jnp.float32)
    key_heads = key_tile.reshape(TOK, HEADS, HD).astype(jnp.float32)
    value_heads = value_tile.reshape(TOK, HEADS, HD).astype(jnp.float32)
    scores = jnp.einsum("qhd,khd->qhk", query_heads, key_heads) * (HD ** -0.5)
    largest = jnp.max(scores, axis=2)
    weights = jnp.exp(scores - largest[:, :, None])
    totals = jnp.sum(weights, axis=2)
    rounded = lax.optimization_barrier(weights.astype(jnp.bfloat16)).astype(jnp.float32)
    numerator = jnp.einsum("qhk,khd->qhd", rounded, value_heads)
    return numerator, largest, totals


def blank_terms():
    return (jnp.zeros((TOK, HEADS, HD), jnp.float32), jnp.zeros((TOK, HEADS), jnp.float32), jnp.zeros((TOK, HEADS), jnp.float32))


def combine_parts(parts, flags):
    peaks = [jnp.where(flag, part[1], NEG_FILL) for part, flag in zip(parts, flags)]
    top_peak = peaks[0]
    for other in peaks[1:]:
        top_peak = jnp.maximum(top_peak, other)
    numer = jnp.zeros((TOK, HEADS, HD), jnp.float32)
    denom = jnp.zeros((TOK, HEADS), jnp.float32)
    for part, flag in zip(parts, flags):
        factor = jnp.where(flag, jnp.exp(jnp.where(flag, part[1], top_peak) - top_peak), 0.0)
        numer = numer + factor[:, :, None] * part[0]
        denom = denom + factor * part[2]
    return (numer / denom[:, :, None]).astype(jnp.bfloat16).reshape(TOK, HH)


def pixel_shuffle(attended):
    half_grid = GRID // 2
    return attended.reshape(half_grid, 2, half_grid, 2, HH).transpose(0, 2, 1, 3, 4).reshape(half_grid * half_grid, 4 * HH)


def page_layout(page_info):
    columns = page_info[:, 0]
    tile_totals = columns * page_info[:, 1]
    thumbs = page_info[:, 2]
    texts = page_info[:, 3]
    firsts = page_info[:, 4]
    lengths = texts + (tile_totals + 1) * SHUF
    starts = jnp.cumsum(lengths) - lengths
    return columns, tile_totals, thumbs, texts, starts, firsts


def reference(queries, keys, values, page_info):
    columns, tile_totals, thumbs, texts, starts, firsts = page_layout(page_info)

    def slot_rows(position):
        page_index = position // SLOTS
        slot_index = position % SLOTS
        grid_width = columns[page_index]
        tile_total = tile_totals[page_index]
        thumb_slot = thumbs[page_index]
        grid_pos = slot_index - firsts[page_index]
        is_tile = (grid_pos >= 0) & (grid_pos < tile_total)
        has_left = is_tile & (grid_pos % grid_width > 0)
        has_right = is_tile & (grid_pos % grid_width < grid_width - 1)
        left_slot = jnp.maximum(slot_index - 1, 0)
        right_slot = jnp.minimum(slot_index + 1, SLOTS - 1)
        query_tile = queries[page_index, slot_index]
        self_terms = block_terms(query_tile, keys[page_index, slot_index], values[page_index, slot_index])
        left_terms = lax.cond(has_left, lambda: block_terms(query_tile, keys[page_index, left_slot], values[page_index, left_slot]), blank_terms)
        right_terms = lax.cond(has_right, lambda: block_terms(query_tile, keys[page_index, right_slot], values[page_index, right_slot]), blank_terms)
        thumb_terms = lax.cond(is_tile, lambda: block_terms(query_tile, keys[page_index, thumb_slot], values[page_index, thumb_slot]), blank_terms)
        attended = combine_parts((self_terms, left_terms, right_terms, thumb_terms), (jnp.array(True), has_left, has_right, is_tile))
        return pixel_shuffle(attended)

    positions = jnp.arange(PAGES * SLOTS, dtype=jnp.int32)
    shuffled = lax.map(slot_rows, positions)
    page_ids = positions // SLOTS
    slot_ids = positions % SLOTS
    grid_ids = slot_ids - firsts[page_ids]
    is_thumb = slot_ids == thumbs[page_ids]
    is_live = ((grid_ids >= 0) & (grid_ids < tile_totals[page_ids])) | is_thumb
    row_start = starts[page_ids] + texts[page_ids] + jnp.where(is_thumb, tile_totals[page_ids], grid_ids) * SHUF
    shard_total = PAGES * SLOTS
    targets = row_start[:, None] + jnp.arange(SHUF, dtype=jnp.int32)[None, :]
    targets = jnp.where(is_live[:, None], targets, LLM_ROWS * shard_total)
    packed = jnp.zeros((LLM_ROWS * shard_total, 4 * HH), jnp.bfloat16)
    packed = packed.at[targets.reshape(-1)].set(shuffled.reshape(-1, 4 * HH), mode="drop")
    return packed.reshape(LLM_ROWS, shard_total, 4 * HH).transpose(1, 0, 2).reshape(shard_total * LLM_ROWS, 4 * HH)
```

```python
import jax
import jax.numpy as jnp
from jax import lax
from jax.experimental import pallas as pl
from jax.experimental.pallas import tpu as pltpu
from jax.sharding import PartitionSpec as P

HEADS = 13
HD = 128
GRID = 32
TXTMAX = 256
HH = 1664
TOK = 1024
SHUF = 256
QROWS = 512


def passed_along(value, axis, steps):
    count = lax.axis_size(axis)
    initial, last = (max(0, -steps), min(count, count - steps))
    return lax.ppermute(value, axis, [(source, source + steps) for source in range(initial, last)])


def spread(array, axis, root):
    mine = lax.axis_index(axis) == root
    return lax.psum(jnp.where(mine, array, jnp.zeros_like(array)), axis)


def attention_kernel(flags_ref, q_ref, k0, v0, k1, v1, k2, v2, k3, v3, o_ref, acc_ref, top_ref, sum_ref):
    query = q_ref[...]

    def terms(k_ref, v_ref):
        scores = lax.dot_general(
            query, k_ref[...], (((1,), (1,)), ((), ())), preferred_element_type=jnp.float32
        ) * HD ** (-0.5)
        largest = jnp.max(scores, axis=1, keepdims=True)
        weights = jnp.exp(scores - largest)
        totals = jnp.sum(weights, axis=1, keepdims=True)
        numerator = jnp.dot(weights.astype(jnp.bfloat16), v_ref[...], preferred_element_type=jnp.float32)
        return numerator, largest, totals

    numerator, largest, totals = terms(k0, v0)
    acc_ref[...] = numerator
    top_ref[...] = largest
    sum_ref[...] = totals

    for index, (k_ref, v_ref) in enumerate(((k1, v1), (k2, v2), (k3, v3))):

        @pl.when(flags_ref[index] != 0)
        def _(k_ref=k_ref, v_ref=v_ref):
            numerator, largest, totals = terms(k_ref, v_ref)
            old_top = top_ref[...]
            new_top = jnp.maximum(old_top, largest)
            keep = jnp.exp(old_top - new_top)
            take = jnp.exp(largest - new_top)
            acc_ref[...] = acc_ref[...] * keep + numerator * take
            sum_ref[...] = sum_ref[...] * keep + totals * take
            top_ref[...] = new_top

    o_ref[...] = (acc_ref[...] / sum_ref[...]).astype(o_ref.dtype)


def attend(flags, query_tile, blocks):
    row_spec = pl.BlockSpec((QROWS, HD), lambda h, i, flags: (i, h))
    col_spec = pl.BlockSpec((TOK, HD), lambda h, i, flags: (0, h))
    operands = []
    for key_tile, value_tile in blocks:
        operands += [key_tile, value_tile]
    return pl.pallas_call(
        attention_kernel,
        grid_spec=pltpu.PrefetchScalarGridSpec(
            num_scalar_prefetch=1,
            grid=(HEADS, TOK // QROWS),
            in_specs=[row_spec] + [col_spec] * len(operands),
            out_specs=row_spec,
            scratch_shapes=[
                pltpu.VMEM((QROWS, HD), jnp.float32),
                pltpu.VMEM((QROWS, 1), jnp.float32),
                pltpu.VMEM((QROWS, 1), jnp.float32),
            ],
        ),
        out_shape=jax.ShapeDtypeStruct((TOK, HH), jnp.bfloat16),
    )(flags, query_tile, *operands)


def pixel_shuffle(attended):
    half_grid = GRID // 2
    return (
        attended.reshape(half_grid, 2, half_grid, 2, HH)
        .transpose(0, 2, 1, 3, 4)
        .reshape(half_grid * half_grid, 4 * HH)
    )


def page_layout(page_info):
    columns = page_info[:, 0]
    tile_totals = columns * page_info[:, 1]
    thumbs = page_info[:, 2]
    texts = page_info[:, 3]
    firsts = page_info[:, 4]
    lengths = texts + (tile_totals + 1) * SHUF
    starts = jnp.cumsum(lengths) - lengths
    return (columns, tile_totals, thumbs, texts, starts, firsts)


def body(queries, keys, values, page_info):
    query_tile = queries.reshape(TOK, HH)
    key_tile = keys.reshape(TOK, HH)
    value_tile = values.reshape(TOK, HH)
    slot_count = lax.axis_size("tile")
    page_count = lax.axis_size("dp")
    device_count = page_count * slot_count
    page_index = lax.axis_index("dp")
    slot_index = lax.axis_index("tile")
    columns, tile_totals, thumbs, texts, starts, firsts = page_layout(page_info)
    grid_width = columns[page_index]
    tile_total = tile_totals[page_index]
    thumb_slot = thumbs[page_index]
    grid_pos = slot_index - firsts[page_index]
    is_tile = (grid_pos >= 0) & (grid_pos < tile_total)
    has_left = is_tile & (grid_pos % grid_width > 0)
    has_right = is_tile & (grid_pos % grid_width < grid_width - 1)
    left_keys, left_values = passed_along((key_tile, value_tile), "tile", 1)
    right_keys, right_values = passed_along((key_tile, value_tile), "tile", -1)
    thumb_keys, thumb_values = (
        spread(key_tile, "tile", thumb_slot),
        spread(value_tile, "tile", thumb_slot),
    )
    flags = jnp.stack([has_left, has_right, is_tile]).astype(jnp.int32)
    attended = attend(
        flags,
        query_tile,
        (
            (key_tile, value_tile),
            (left_keys, left_values),
            (right_keys, right_values),
            (thumb_keys, thumb_values),
        ),
    )
    shuffled = pixel_shuffle(attended)
    is_thumb = slot_index == thumb_slot
    is_live = is_tile | is_thumb
    row_start = (
        starts[page_index] + texts[page_index] + jnp.where(is_thumb, tile_total, grid_pos) * SHUF
    )
    per_peer = SHUF // device_count
    arranged = jnp.roll(
        shuffled.reshape(per_peer, device_count, 4 * HH), row_start % device_count, axis=1
    )
    arranged = jnp.where(is_live, arranged, jnp.zeros_like(arranged))
    arrived = lax.all_to_all(arranged, ("dp", "tile"), split_axis=1, concat_axis=1, tiled=True)
    own_rank = page_index * slot_count + slot_index
    sources = jnp.arange(device_count, dtype=jnp.int32)
    source_page = sources // slot_count
    source_slot = sources % slot_count
    source_grid = source_slot - firsts[source_page]
    source_thumb = source_slot == thumbs[source_page]
    source_live = (source_grid >= 0) & (source_grid < tile_totals[source_page]) | source_thumb
    source_start = (
        starts[source_page]
        + texts[source_page]
        + jnp.where(source_thumb, tile_totals[source_page], source_grid) * SHUF
    )
    first_row = (source_start + (own_rank - source_start) % device_count) // device_count
    shard_rows = SHUF + TXTMAX // slot_count
    targets = first_row[None, :] + jnp.arange(per_peer, dtype=jnp.int32)[:, None]
    targets = jnp.where(source_live[None, :], targets, shard_rows)
    placed = jnp.zeros((shard_rows, 4 * HH), jnp.bfloat16)
    return placed.at[targets.reshape(-1)].set(arrived.reshape(-1, 4 * HH), mode="drop")


def solution(mesh):
    placed = (
        P("dp", "tile", None, None),
        P("dp", "tile", None, None),
        P("dp", "tile", None, None),
        P(),
    )
    return jax.shard_map(
        body, mesh=mesh, in_specs=placed, out_specs=P(("dp", "tile"), None), check_vma=False
    )
```

```python
import jax
import jax.numpy as jnp
from jax import lax
from jax.experimental import pallas as pl
from jax.experimental.pallas import tpu as pltpu
from jax.sharding import PartitionSpec as P

HEADS = 13
HD = 128
GRID = 32
TXTMAX = 256
HH = 1664
TOK = 1024
SHUF = 256
HEAD_CHUNKS = ((0, 4), (4, 8), (8, 13))


def passed_along(value, axis, steps):
    count = lax.axis_size(axis)
    initial, last = (max(0, -steps), min(count, count - steps))
    return lax.ppermute(value, axis, [(source, source + steps) for source in range(initial, last)])


def attention_kernel(flags_ref, q_ref, k0, v0, k1, v1, k2, v2, k3, v3, o_ref, acc_ref, top_ref, sum_ref):
    query = q_ref[...]
    ones = jnp.ones((TOK, HD), jnp.bfloat16)

    def terms(k_ref, v_ref):
        scores = lax.dot_general(
            query, k_ref[...], (((1,), (1,)), ((), ())), preferred_element_type=jnp.float32
        ) * HD ** (-0.5)
        largest = jnp.max(scores, axis=1, keepdims=True)
        weights = jnp.exp(scores - largest).astype(jnp.bfloat16)
        both = jnp.dot(
            weights, jnp.concatenate([v_ref[...], ones], axis=1), preferred_element_type=jnp.float32
        )
        return both[:, :HD], largest, both[:, HD : HD + 1]

    numerator, largest, totals = terms(k0, v0)
    acc_ref[...] = numerator
    top_ref[...] = largest
    sum_ref[...] = totals

    for index, (k_ref, v_ref) in enumerate(((k1, v1), (k2, v2), (k3, v3))):

        @pl.when(flags_ref[index] != 0)
        def _(k_ref=k_ref, v_ref=v_ref):
            numerator, largest, totals = terms(k_ref, v_ref)
            old_top = top_ref[...]
            new_top = jnp.maximum(old_top, largest)
            keep = jnp.exp(old_top - new_top)
            take = jnp.exp(largest - new_top)
            acc_ref[...] = acc_ref[...] * keep + numerator * take
            sum_ref[...] = sum_ref[...] * keep + totals * take
            top_ref[...] = new_top

    o_ref[...] = (acc_ref[...] / sum_ref[...]).astype(o_ref.dtype)


def attend(flags, query_cols, blocks, head_count):
    q_spec = pl.BlockSpec((TOK, HD), lambda h, flags: (0, h))
    k_spec = pl.BlockSpec((TOK, HD), lambda h, flags: (0, h))
    v_spec = pl.BlockSpec((TOK, HD), lambda h, flags: (0, head_count + h))
    operands = []
    for both in blocks:
        operands += [both, both]
    return pl.pallas_call(
        attention_kernel,
        grid_spec=pltpu.PrefetchScalarGridSpec(
            num_scalar_prefetch=1,
            grid=(head_count,),
            in_specs=[q_spec] + [k_spec, v_spec] * len(blocks),
            out_specs=q_spec,
            scratch_shapes=[
                pltpu.VMEM((TOK, HD), jnp.float32),
                pltpu.VMEM((TOK, 1), jnp.float32),
                pltpu.VMEM((TOK, 1), jnp.float32),
            ],
        ),
        out_shape=jax.ShapeDtypeStruct((TOK, head_count * HD), jnp.bfloat16),
    )(flags, query_cols, *operands)


def pixel_shuffle(attended):
    half_grid = GRID // 2
    width = attended.shape[-1]
    return (
        attended.reshape(half_grid, 2, half_grid, 2, width)
        .transpose(0, 2, 1, 3, 4)
        .reshape(half_grid * half_grid, 4 * width)
    )


def page_layout(page_info):
    columns = page_info[:, 0]
    tile_totals = columns * page_info[:, 1]
    thumbs = page_info[:, 2]
    texts = page_info[:, 3]
    firsts = page_info[:, 4]
    lengths = texts + (tile_totals + 1) * SHUF
    starts = jnp.cumsum(lengths) - lengths
    return (columns, tile_totals, thumbs, texts, starts, firsts)


def body(queries, keys, values, page_info):
    query_tile = queries.reshape(TOK, HH)
    key_tile = keys.reshape(TOK, HH)
    value_tile = values.reshape(TOK, HH)
    slot_count = lax.axis_size("tile")
    page_count = lax.axis_size("dp")
    device_count = page_count * slot_count
    page_index = lax.axis_index("dp")
    slot_index = lax.axis_index("tile")
    columns, tile_totals, thumbs, texts, starts, firsts = page_layout(page_info)
    grid_width = columns[page_index]
    tile_total = tile_totals[page_index]
    thumb_slot = thumbs[page_index]
    grid_pos = slot_index - firsts[page_index]
    is_tile = (grid_pos >= 0) & (grid_pos < tile_total)
    has_left = is_tile & (grid_pos % grid_width > 0)
    has_right = is_tile & (grid_pos % grid_width < grid_width - 1)
    flags = jnp.stack([has_left, has_right, is_tile]).astype(jnp.int32)
    is_thumb = slot_index == thumb_slot
    is_live = is_tile | is_thumb
    row_start = (
        starts[page_index] + texts[page_index] + jnp.where(is_thumb, tile_total, grid_pos) * SHUF
    )
    per_peer = SHUF // device_count

    arrived_parts = []
    previous_thumb = None
    for first_head, end_head in HEAD_CHUNKS:
        head_count = end_head - first_head
        cols = slice(first_head * HD, end_head * HD)
        own = jnp.concatenate([key_tile[:, cols], value_tile[:, cols]], axis=1)
        left = passed_along(own, "tile", 1)
        right = passed_along(own, "tile", -1)
        mine = jnp.where(slot_index == thumb_slot, own, jnp.zeros_like(own))
        if previous_thumb is not None:
            previous_thumb, mine = lax.optimization_barrier((previous_thumb, mine))
        thumb = lax.psum(mine, "tile")
        previous_thumb = thumb
        attended = attend(flags, query_tile[:, cols], (own, left, right, thumb), head_count)
        shuffled = pixel_shuffle(attended)
        arranged = jnp.roll(
            shuffled.reshape(per_peer, device_count, 4 * head_count * HD),
            row_start % device_count,
            axis=1,
        )
        arranged = jnp.where(is_live, arranged, jnp.zeros_like(arranged))
        arrived = lax.all_to_all(arranged, ("dp", "tile"), split_axis=1, concat_axis=1, tiled=True)
        arrived_parts.append(arrived.reshape(per_peer, device_count, 4, head_count * HD))
    arrived = jnp.concatenate(arrived_parts, axis=3).reshape(per_peer, device_count, 4 * HH)

    own_rank = page_index * slot_count + slot_index
    sources = jnp.arange(device_count, dtype=jnp.int32)
    source_page = sources // slot_count
    source_slot = sources % slot_count
    source_grid = source_slot - firsts[source_page]
    source_thumb = source_slot == thumbs[source_page]
    source_live = (source_grid >= 0) & (source_grid < tile_totals[source_page]) | source_thumb
    source_start = (
        starts[source_page]
        + texts[source_page]
        + jnp.where(source_thumb, tile_totals[source_page], source_grid) * SHUF
    )
    first_row = (source_start + (own_rank - source_start) % device_count) // device_count
    shard_rows = SHUF + TXTMAX // slot_count
    targets = first_row[None, :] + jnp.arange(per_peer, dtype=jnp.int32)[:, None]
    targets = jnp.where(source_live[None, :], targets, shard_rows)
    placed = jnp.zeros((shard_rows, 4 * HH), jnp.bfloat16)
    return placed.at[targets.reshape(-1)].set(arrived.reshape(-1, 4 * HH), mode="drop")


def solution(mesh):
    placed = (
        P("dp", "tile", None, None),
        P("dp", "tile", None, None),
        P("dp", "tile", None, None),
        P(),
    )
    return jax.shard_map(
        body, mesh=mesh, in_specs=placed, out_specs=P(("dp", "tile"), None), check_vma=False
    )
```

```python
import jax
import jax.numpy as jnp
from jax import lax
from jax.experimental import pallas as pl
from jax.experimental.pallas import tpu as pltpu
from jax.sharding import PartitionSpec as P

HEADS = 13
HD = 128
GRID = 32
TXTMAX = 256
HH = 1664
TOK = 1024
SHUF = 256
HEAD_CHUNKS = ((0, 4), (4, 8), (8, 13))


def passed_along(value, axis, steps):
    count = lax.axis_size(axis)
    initial, last = (max(0, -steps), min(count, count - steps))
    return lax.ppermute(value, axis, [(source, source + steps) for source in range(initial, last)])


def block_terms(query, k_ref, v_ref):
    scores = lax.dot_general(
        query, k_ref[...], (((1,), (1,)), ((), ())), preferred_element_type=jnp.float32
    ) * HD ** (-0.5)
    largest = jnp.max(scores, axis=1, keepdims=True)
    weights = jnp.exp(scores - largest).astype(jnp.bfloat16)
    ones = jnp.ones((TOK, HD), jnp.bfloat16)
    both = jnp.dot(
        weights, jnp.concatenate([v_ref[...], ones], axis=1), preferred_element_type=jnp.float32
    )
    return both[:, :HD], largest, both[:, HD : HD + 1]


def merge_block(flag, query, k_ref, v_ref, acc_ref, top_ref, sum_ref):
    @pl.when(flag != 0)
    def _():
        numerator, largest, totals = block_terms(query, k_ref, v_ref)
        old_top = top_ref[...]
        new_top = jnp.maximum(old_top, largest)
        keep = jnp.exp(old_top - new_top)
        take = jnp.exp(largest - new_top)
        acc_ref[...] = acc_ref[...] * keep + numerator * take
        sum_ref[...] = sum_ref[...] * keep + totals * take
        top_ref[...] = new_top


def near_kernel(flags_ref, q_ref, k0, v0, k1, v1, k2, v2, acc_ref, top_ref, sum_ref):
    query = q_ref[...]
    numerator, largest, totals = block_terms(query, k0, v0)
    acc_ref[...] = numerator
    top_ref[0] = largest
    sum_ref[0] = totals
    merge_block(flags_ref[0], query, k1, v1, acc_ref, top_ref.at[0], sum_ref.at[0])
    merge_block(flags_ref[1], query, k2, v2, acc_ref, top_ref.at[0], sum_ref.at[0])


def thumb_kernel(flags_ref, q_ref, k3, v3, acc_in, top_in, sum_in, o_ref, acc_ref, top_ref, sum_ref):
    acc_ref[...] = acc_in[...]
    top_ref[...] = top_in[0]
    sum_ref[...] = sum_in[0]
    merge_block(flags_ref[2], q_ref[...], k3, v3, acc_ref, top_ref, sum_ref)
    o_ref[...] = (acc_ref[...] / sum_ref[...]).astype(o_ref.dtype)


def attend_near(flags, query_cols, blocks, head_count):
    q_spec = pl.BlockSpec((TOK, HD), lambda h, flags: (0, h))
    v_spec = pl.BlockSpec((TOK, HD), lambda h, flags: (0, head_count + h))
    stat_spec = pl.BlockSpec((1, TOK, 1), lambda h, flags: (h, 0, 0))
    operands = []
    for both in blocks:
        operands += [both, both]
    return pl.pallas_call(
        near_kernel,
        grid_spec=pltpu.PrefetchScalarGridSpec(
            num_scalar_prefetch=1,
            grid=(head_count,),
            in_specs=[q_spec] + [q_spec, v_spec] * len(blocks),
            out_specs=[q_spec, stat_spec, stat_spec],
        ),
        out_shape=[
            jax.ShapeDtypeStruct((TOK, head_count * HD), jnp.float32),
            jax.ShapeDtypeStruct((head_count, TOK, 1), jnp.float32),
            jax.ShapeDtypeStruct((head_count, TOK, 1), jnp.float32),
        ],
    )(flags, query_cols, *operands)


def attend_thumb(flags, query_tile, thumb, acc, top, totals):
    q_spec = pl.BlockSpec((TOK, HD), lambda h, flags: (0, h))
    v_spec = pl.BlockSpec((TOK, HD), lambda h, flags: (0, HEADS + h))
    stat_spec = pl.BlockSpec((1, TOK, 1), lambda h, flags: (h, 0, 0))
    return pl.pallas_call(
        thumb_kernel,
        grid_spec=pltpu.PrefetchScalarGridSpec(
            num_scalar_prefetch=1,
            grid=(HEADS,),
            in_specs=[q_spec, q_spec, v_spec, q_spec, stat_spec, stat_spec],
            out_specs=q_spec,
            scratch_shapes=[
                pltpu.VMEM((TOK, HD), jnp.float32),
                pltpu.VMEM((TOK, 1), jnp.float32),
                pltpu.VMEM((TOK, 1), jnp.float32),
            ],
        ),
        out_shape=jax.ShapeDtypeStruct((TOK, HH), jnp.bfloat16),
    )(flags, query_tile, thumb, thumb, acc, top, totals)


def pixel_shuffle(attended):
    half_grid = GRID // 2
    width = attended.shape[-1]
    return (
        attended.reshape(half_grid, 2, half_grid, 2, width)
        .transpose(0, 2, 1, 3, 4)
        .reshape(half_grid * half_grid, 4 * width)
    )


def page_layout(page_info):
    columns = page_info[:, 0]
    tile_totals = columns * page_info[:, 1]
    thumbs = page_info[:, 2]
    texts = page_info[:, 3]
    firsts = page_info[:, 4]
    lengths = texts + (tile_totals + 1) * SHUF
    starts = jnp.cumsum(lengths) - lengths
    return (columns, tile_totals, thumbs, texts, starts, firsts)


def body(queries, keys, values, page_info):
    query_tile = queries.reshape(TOK, HH)
    key_tile = keys.reshape(TOK, HH)
    value_tile = values.reshape(TOK, HH)
    slot_count = lax.axis_size("tile")
    page_count = lax.axis_size("dp")
    device_count = page_count * slot_count
    page_index = lax.axis_index("dp")
    slot_index = lax.axis_index("tile")
    columns, tile_totals, thumbs, texts, starts, firsts = page_layout(page_info)
    grid_width = columns[page_index]
    tile_total = tile_totals[page_index]
    thumb_slot = thumbs[page_index]
    grid_pos = slot_index - firsts[page_index]
    is_tile = (grid_pos >= 0) & (grid_pos < tile_total)
    has_left = is_tile & (grid_pos % grid_width > 0)
    has_right = is_tile & (grid_pos % grid_width < grid_width - 1)
    flags = jnp.stack([has_left, has_right, is_tile]).astype(jnp.int32)
    is_thumb = slot_index == thumb_slot
    is_live = is_tile | is_thumb
    row_start = (
        starts[page_index] + texts[page_index] + jnp.where(is_thumb, tile_total, grid_pos) * SHUF
    )
    per_peer = SHUF // device_count

    mine = jnp.where(
        slot_index == thumb_slot,
        jnp.concatenate([key_tile, value_tile], axis=1),
        jnp.zeros((TOK, 2 * HH), jnp.bfloat16),
    )
    thumb = lax.psum(mine, "tile")
    states = []
    for first_head, end_head in HEAD_CHUNKS:
        head_count = end_head - first_head
        cols = slice(first_head * HD, end_head * HD)
        own = jnp.concatenate([key_tile[:, cols], value_tile[:, cols]], axis=1)
        left = passed_along(own, "tile", 1)
        right = passed_along(own, "tile", -1)
        states.append(attend_near(flags, query_tile[:, cols], (own, left, right), head_count))
    acc, top, totals = (jnp.concatenate(parts, axis=axis) for parts, axis in zip(zip(*states), (1, 0, 0)))
    attended = attend_thumb(flags, query_tile, thumb, acc, top, totals)
    shuffled = pixel_shuffle(attended)
    arranged = jnp.roll(
        shuffled.reshape(per_peer, device_count, 4 * HH), row_start % device_count, axis=1
    )
    arranged = jnp.where(is_live, arranged, jnp.zeros_like(arranged))
    arrived = lax.all_to_all(arranged, ("dp", "tile"), split_axis=1, concat_axis=1, tiled=True)
    own_rank = page_index * slot_count + slot_index
    sources = jnp.arange(device_count, dtype=jnp.int32)
    source_page = sources // slot_count
    source_slot = sources % slot_count
    source_grid = source_slot - firsts[source_page]
    source_thumb = source_slot == thumbs[source_page]
    source_live = (source_grid >= 0) & (source_grid < tile_totals[source_page]) | source_thumb
    source_start = (
        starts[source_page]
        + texts[source_page]
        + jnp.where(source_thumb, tile_totals[source_page], source_grid) * SHUF
    )
    first_row = (source_start + (own_rank - source_start) % device_count) // device_count
    shard_rows = SHUF + TXTMAX // slot_count
    targets = first_row[None, :] + jnp.arange(per_peer, dtype=jnp.int32)[:, None]
    targets = jnp.where(source_live[None, :], targets, shard_rows)
    placed = jnp.zeros((shard_rows, 4 * HH), jnp.bfloat16)
    return placed.at[targets.reshape(-1)].set(arrived.reshape(-1, 4 * HH), mode="drop")


def solution(mesh):
    placed = (
        P("dp", "tile", None, None),
        P("dp", "tile", None, None),
        P("dp", "tile", None, None),
        P(),
    )
    return jax.shard_map(
        body, mesh=mesh, in_specs=placed, out_specs=P(("dp", "tile"), None), check_vma=False
    )
```

```python
import jax
import jax.numpy as jnp
from jax import lax
from jax.experimental import pallas as pl
from jax.experimental.pallas import tpu as pltpu
from jax.sharding import PartitionSpec as P

HEADS = 13
HD = 128
GRID = 32
TXTMAX = 256
HH = 1664
TOK = 1024
SHUF = 256
HEAD_CHUNKS = ((0, 4), (4, 8), (8, 13))


def passed_along(value, axis, steps):
    count = lax.axis_size(axis)
    initial, last = (max(0, -steps), min(count, count - steps))
    return lax.ppermute(value, axis, [(source, source + steps) for source in range(initial, last)])


def block_terms(query, k_ref, v_ref):
    scores = lax.dot_general(
        query, k_ref[...], (((1,), (1,)), ((), ())), preferred_element_type=jnp.float32
    ) * HD ** (-0.5)
    largest = jnp.max(scores, axis=1, keepdims=True)
    weights = jnp.exp(scores - largest).astype(jnp.bfloat16)
    ones = jnp.ones((TOK, HD), jnp.bfloat16)
    both = jnp.dot(
        weights, jnp.concatenate([v_ref[...], ones], axis=1), preferred_element_type=jnp.float32
    )
    return both[:, :HD], largest, both[:, HD : HD + 1]


def merge_block(flag, query, k_ref, v_ref, acc_ref, top_ref, sum_ref):
    @pl.when(flag != 0)
    def _():
        numerator, largest, totals = block_terms(query, k_ref, v_ref)
        old_top = top_ref[...]
        new_top = jnp.maximum(old_top, largest)
        keep = jnp.exp(old_top - new_top)
        take = jnp.exp(largest - new_top)
        acc_ref[...] = acc_ref[...] * keep + numerator * take
        sum_ref[...] = sum_ref[...] * keep + totals * take
        top_ref[...] = new_top


def near_kernel(flags_ref, q_ref, k0, v0, k1, v1, k2, v2, acc_prev, top_prev, sum_prev, acc_ref, top_ref, sum_ref):
    query = q_ref[...]
    numerator, largest, totals = block_terms(query, k0, v0)
    acc_ref[...] = numerator
    top_ref[0] = largest
    sum_ref[0] = totals
    merge_block(flags_ref[0], query, k1, v1, acc_ref, top_ref.at[0], sum_ref.at[0])
    merge_block(flags_ref[1], query, k2, v2, acc_ref, top_ref.at[0], sum_ref.at[0])


def thumb_kernel(flags_ref, q_ref, k3, v3, acc_in, top_in, sum_in, o_ref, acc_ref, top_ref, sum_ref):
    acc_ref[...] = acc_in[...]
    top_ref[...] = top_in[0]
    sum_ref[...] = sum_in[0]
    merge_block(flags_ref[2], q_ref[...], k3, v3, acc_ref, top_ref, sum_ref)
    o_ref[...] = (acc_ref[...] / sum_ref[...]).astype(o_ref.dtype)


def attend_near(flags, query_cols, blocks, first_head, head_count, state):
    q_spec = pl.BlockSpec((TOK, HD), lambda h, flags: (0, h))
    v_spec = pl.BlockSpec((TOK, HD), lambda h, flags: (0, head_count + h))
    acc_spec = pl.BlockSpec((TOK, HD), lambda h, flags: (0, first_head + h))
    stat_spec = pl.BlockSpec((1, TOK, 1), lambda h, flags: (first_head + h, 0, 0))
    held = pl.BlockSpec(memory_space=pl.ANY)
    operands = []
    for both in blocks:
        operands += [both, both]
    count = 1 + len(operands)
    return pl.pallas_call(
        near_kernel,
        grid_spec=pltpu.PrefetchScalarGridSpec(
            num_scalar_prefetch=1,
            grid=(head_count,),
            in_specs=[q_spec] + [q_spec, v_spec] * len(blocks) + [held] * 3,
            out_specs=[acc_spec, stat_spec, stat_spec],
        ),
        out_shape=[
            jax.ShapeDtypeStruct((TOK, HH), jnp.float32),
            jax.ShapeDtypeStruct((HEADS, TOK, 1), jnp.float32),
            jax.ShapeDtypeStruct((HEADS, TOK, 1), jnp.float32),
        ],
        input_output_aliases={count + 1: 0, count + 2: 1, count + 3: 2},
    )(flags, query_cols, *operands, *state)


def attend_thumb(flags, query_tile, thumb_keys, thumb_values, acc, top, totals):
    q_spec = pl.BlockSpec((TOK, HD), lambda h, flags: (0, h))
    stat_spec = pl.BlockSpec((1, TOK, 1), lambda h, flags: (h, 0, 0))
    return pl.pallas_call(
        thumb_kernel,
        grid_spec=pltpu.PrefetchScalarGridSpec(
            num_scalar_prefetch=1,
            grid=(HEADS,),
            in_specs=[q_spec, q_spec, q_spec, q_spec, stat_spec, stat_spec],
            out_specs=q_spec,
            scratch_shapes=[
                pltpu.VMEM((TOK, HD), jnp.float32),
                pltpu.VMEM((TOK, 1), jnp.float32),
                pltpu.VMEM((TOK, 1), jnp.float32),
            ],
        ),
        out_shape=jax.ShapeDtypeStruct((TOK, HH), jnp.bfloat16),
    )(flags, query_tile, thumb_keys, thumb_values, acc, top, totals)


def pixel_shuffle(attended):
    half_grid = GRID // 2
    width = attended.shape[-1]
    return (
        attended.reshape(half_grid, 2, half_grid, 2, width)
        .transpose(0, 2, 1, 3, 4)
        .reshape(half_grid * half_grid, 4 * width)
    )


def page_layout(page_info):
    columns = page_info[:, 0]
    tile_totals = columns * page_info[:, 1]
    thumbs = page_info[:, 2]
    texts = page_info[:, 3]
    firsts = page_info[:, 4]
    lengths = texts + (tile_totals + 1) * SHUF
    starts = jnp.cumsum(lengths) - lengths
    return (columns, tile_totals, thumbs, texts, starts, firsts)


def body(queries, keys, values, page_info):
    query_tile = queries.reshape(TOK, HH)
    key_tile = keys.reshape(TOK, HH)
    value_tile = values.reshape(TOK, HH)
    slot_count = lax.axis_size("tile")
    page_count = lax.axis_size("dp")
    device_count = page_count * slot_count
    page_index = lax.axis_index("dp")
    slot_index = lax.axis_index("tile")
    columns, tile_totals, thumbs, texts, starts, firsts = page_layout(page_info)
    grid_width = columns[page_index]
    tile_total = tile_totals[page_index]
    thumb_slot = thumbs[page_index]
    grid_pos = slot_index - firsts[page_index]
    is_tile = (grid_pos >= 0) & (grid_pos < tile_total)
    has_left = is_tile & (grid_pos % grid_width > 0)
    has_right = is_tile & (grid_pos % grid_width < grid_width - 1)
    flags = jnp.stack([has_left, has_right, is_tile]).astype(jnp.int32)
    is_thumb = slot_index == thumb_slot
    is_live = is_tile | is_thumb
    row_start = (
        starts[page_index] + texts[page_index] + jnp.where(is_thumb, tile_total, grid_pos) * SHUF
    )
    per_peer = SHUF // device_count

    mine = slot_index == thumb_slot
    thumb_keys = lax.psum(jnp.where(mine, key_tile, jnp.zeros_like(key_tile)), "tile")
    thumb_values = lax.psum(jnp.where(mine, value_tile, jnp.zeros_like(value_tile)), "tile")
    state = (
        jnp.zeros((TOK, HH), jnp.float32),
        jnp.zeros((HEADS, TOK, 1), jnp.float32),
        jnp.zeros((HEADS, TOK, 1), jnp.float32),
    )
    for first_head, end_head in HEAD_CHUNKS:
        head_count = end_head - first_head
        cols = slice(first_head * HD, end_head * HD)
        own = jnp.concatenate([key_tile[:, cols], value_tile[:, cols]], axis=1)
        left = passed_along(own, "tile", 1)
        right = passed_along(own, "tile", -1)
        state = attend_near(
            flags, query_tile[:, cols], (own, left, right), first_head, head_count, state
        )
    attended = attend_thumb(flags, query_tile, thumb_keys, thumb_values, *state)
    shuffled = pixel_shuffle(attended)
    arranged = jnp.roll(
        shuffled.reshape(per_peer, device_count, 4 * HH), row_start % device_count, axis=1
    )
    arranged = jnp.where(is_live, arranged, jnp.zeros_like(arranged))
    arrived = lax.all_to_all(arranged, ("dp", "tile"), split_axis=1, concat_axis=1, tiled=True)
    own_rank = page_index * slot_count + slot_index
    sources = jnp.arange(device_count, dtype=jnp.int32)
    source_page = sources // slot_count
    source_slot = sources % slot_count
    source_grid = source_slot - firsts[source_page]
    source_thumb = source_slot == thumbs[source_page]
    source_live = (source_grid >= 0) & (source_grid < tile_totals[source_page]) | source_thumb
    source_start = (
        starts[source_page]
        + texts[source_page]
        + jnp.where(source_thumb, tile_totals[source_page], source_grid) * SHUF
    )
    first_row = (source_start + (own_rank - source_start) % device_count) // device_count
    shard_rows = SHUF + TXTMAX // slot_count
    targets = first_row[None, :] + jnp.arange(per_peer, dtype=jnp.int32)[:, None]
    targets = jnp.where(source_live[None, :], targets, shard_rows)
    placed = jnp.zeros((shard_rows, 4 * HH), jnp.bfloat16)
    return placed.at[targets.reshape(-1)].set(arrived.reshape(-1, 4 * HH), mode="drop")


def solution(mesh):
    placed = (
        P("dp", "tile", None, None),
        P("dp", "tile", None, None),
        P("dp", "tile", None, None),
        P(),
    )
    return jax.shard_map(
        body, mesh=mesh, in_specs=placed, out_specs=P(("dp", "tile"), None), check_vma=False
    )
```

```python
import jax
import jax.numpy as jnp
from jax import lax
from jax.experimental import pallas as pl
from jax.experimental.pallas import tpu as pltpu
from jax.sharding import PartitionSpec as P

HEADS = 13
HD = 128
GRID = 32
TXTMAX = 256
HH = 1664
TOK = 1024
SHUF = 256
HEAD_CHUNKS = ((0, 4), (4, 8), (8, 13))


def passed_along(value, axis, steps):
    count = lax.axis_size(axis)
    initial, last = (max(0, -steps), min(count, count - steps))
    return lax.ppermute(value, axis, [(source, source + steps) for source in range(initial, last)])


def block_terms(query, k_ref, v_ref):
    scores = lax.dot_general(
        query, k_ref[...], (((1,), (1,)), ((), ())), preferred_element_type=jnp.float32
    ) * HD ** (-0.5)
    largest = jnp.max(scores, axis=1, keepdims=True)
    weights = jnp.exp(scores - largest).astype(jnp.bfloat16)
    ones = jnp.ones((TOK, HD), jnp.bfloat16)
    both = jnp.dot(
        weights, jnp.concatenate([v_ref[...], ones], axis=1), preferred_element_type=jnp.float32
    )
    return both[:, :HD], largest, both[:, HD : HD + 1]


def merge_block(flag, query, k_ref, v_ref, acc_ref, top_ref, sum_ref):
    @pl.when(flag != 0)
    def _():
        numerator, largest, totals = block_terms(query, k_ref, v_ref)
        old_top = top_ref[...]
        new_top = jnp.maximum(old_top, largest)
        keep = jnp.exp(old_top - new_top)
        take = jnp.exp(largest - new_top)
        acc_ref[...] = acc_ref[...] * keep + numerator * take
        sum_ref[...] = sum_ref[...] * keep + totals * take
        top_ref[...] = new_top


def near_kernel(flags_ref, q_ref, k0, v0, k1, v1, k2, v2, acc_prev, top_prev, sum_prev, acc_ref, top_ref, sum_ref):
    query = q_ref[...]
    numerator, largest, totals = block_terms(query, k0, v0)
    acc_ref[...] = numerator
    top_ref[0] = largest
    sum_ref[0] = totals
    merge_block(flags_ref[0], query, k1, v1, acc_ref, top_ref.at[0], sum_ref.at[0])
    merge_block(flags_ref[1], query, k2, v2, acc_ref, top_ref.at[0], sum_ref.at[0])


def thumb_kernel(flags_ref, q_ref, k3, v3, acc_in, top_in, sum_in, o_ref, acc_ref, top_ref, sum_ref):
    acc_ref[...] = acc_in[...]
    top_ref[...] = top_in[0]
    sum_ref[...] = sum_in[0]
    merge_block(flags_ref[2], q_ref[...], k3, v3, acc_ref, top_ref, sum_ref)
    o_ref[...] = (acc_ref[...] / sum_ref[...]).astype(o_ref.dtype)


def attend_near(flags, query_cols, blocks, first_head, head_count, state):
    q_spec = pl.BlockSpec((TOK, HD), lambda h, flags: (0, h))
    v_spec = pl.BlockSpec((TOK, HD), lambda h, flags: (0, head_count + h))
    acc_spec = pl.BlockSpec((TOK, HD), lambda h, flags: (0, first_head + h))
    stat_spec = pl.BlockSpec((1, TOK, 1), lambda h, flags: (first_head + h, 0, 0))
    held = pl.BlockSpec(memory_space=pl.ANY)
    operands = []
    for both in blocks:
        operands += [both, both]
    count = 1 + len(operands)
    return pl.pallas_call(
        near_kernel,
        grid_spec=pltpu.PrefetchScalarGridSpec(
            num_scalar_prefetch=1,
            grid=(head_count,),
            in_specs=[q_spec] + [q_spec, v_spec] * len(blocks) + [held] * 3,
            out_specs=[acc_spec, stat_spec, stat_spec],
        ),
        out_shape=[
            jax.ShapeDtypeStruct((TOK, HH), jnp.float32),
            jax.ShapeDtypeStruct((HEADS, TOK, 1), jnp.float32),
            jax.ShapeDtypeStruct((HEADS, TOK, 1), jnp.float32),
        ],
        input_output_aliases={count + 1: 0, count + 2: 1, count + 3: 2},
    )(flags, query_cols, *operands, *state)


def attend_thumb(flags, query_tile, thumb_keys, thumb_values, acc, top, totals):
    q_spec = pl.BlockSpec((TOK, HD), lambda h, flags: (0, h))
    stat_spec = pl.BlockSpec((1, TOK, 1), lambda h, flags: (h, 0, 0))
    return pl.pallas_call(
        thumb_kernel,
        grid_spec=pltpu.PrefetchScalarGridSpec(
            num_scalar_prefetch=1,
            grid=(HEADS,),
            in_specs=[q_spec, q_spec, q_spec, q_spec, stat_spec, stat_spec],
            out_specs=q_spec,
            scratch_shapes=[
                pltpu.VMEM((TOK, HD), jnp.float32),
                pltpu.VMEM((TOK, 1), jnp.float32),
                pltpu.VMEM((TOK, 1), jnp.float32),
            ],
        ),
        out_shape=jax.ShapeDtypeStruct((TOK, HH), jnp.bfloat16),
    )(flags, query_tile, thumb_keys, thumb_values, acc, top, totals)


def pixel_shuffle(attended):
    half_grid = GRID // 2
    width = attended.shape[-1]
    return (
        attended.reshape(half_grid, 2, half_grid, 2, width)
        .transpose(0, 2, 1, 3, 4)
        .reshape(half_grid * half_grid, 4 * width)
    )


def page_layout(page_info):
    columns = page_info[:, 0]
    tile_totals = columns * page_info[:, 1]
    thumbs = page_info[:, 2]
    texts = page_info[:, 3]
    firsts = page_info[:, 4]
    lengths = texts + (tile_totals + 1) * SHUF
    starts = jnp.cumsum(lengths) - lengths
    return (columns, tile_totals, thumbs, texts, starts, firsts)


def body(queries, keys, values, page_info):
    query_tile = queries.reshape(TOK, HH)
    key_tile = keys.reshape(TOK, HH)
    value_tile = values.reshape(TOK, HH)
    slot_count = lax.axis_size("tile")
    page_count = lax.axis_size("dp")
    device_count = page_count * slot_count
    page_index = lax.axis_index("dp")
    slot_index = lax.axis_index("tile")
    columns, tile_totals, thumbs, texts, starts, firsts = page_layout(page_info)
    grid_width = columns[page_index]
    tile_total = tile_totals[page_index]
    thumb_slot = thumbs[page_index]
    grid_pos = slot_index - firsts[page_index]
    is_tile = (grid_pos >= 0) & (grid_pos < tile_total)
    has_left = is_tile & (grid_pos % grid_width > 0)
    has_right = is_tile & (grid_pos % grid_width < grid_width - 1)
    flags = jnp.stack([has_left, has_right, is_tile]).astype(jnp.int32)
    is_thumb = slot_index == thumb_slot
    is_live = is_tile | is_thumb
    row_start = (
        starts[page_index] + texts[page_index] + jnp.where(is_thumb, tile_total, grid_pos) * SHUF
    )
    per_peer = SHUF // device_count
    query_tile = jnp.roll(
        pixel_shuffle(query_tile).reshape(per_peer, device_count, 4 * HH),
        row_start % device_count,
        axis=1,
    ).reshape(TOK, HH)

    mine = slot_index == thumb_slot
    thumb_keys = lax.psum(jnp.where(mine, key_tile, jnp.zeros_like(key_tile)), "tile")
    thumb_values = lax.psum(jnp.where(mine, value_tile, jnp.zeros_like(value_tile)), "tile")
    state = (
        jnp.zeros((TOK, HH), jnp.float32),
        jnp.zeros((HEADS, TOK, 1), jnp.float32),
        jnp.zeros((HEADS, TOK, 1), jnp.float32),
    )
    for first_head, end_head in HEAD_CHUNKS:
        head_count = end_head - first_head
        cols = slice(first_head * HD, end_head * HD)
        own = jnp.concatenate([key_tile[:, cols], value_tile[:, cols]], axis=1)
        left = passed_along(own, "tile", 1)
        right = passed_along(own, "tile", -1)
        state = attend_near(
            flags, query_tile[:, cols], (own, left, right), first_head, head_count, state
        )
    attended = attend_thumb(flags, query_tile, thumb_keys, thumb_values, *state)
    arranged = attended.reshape(per_peer, device_count, 4 * HH)
    arranged = jnp.where(is_live, arranged, jnp.zeros_like(arranged))
    arrived = lax.all_to_all(arranged, ("dp", "tile"), split_axis=1, concat_axis=1, tiled=True)
    own_rank = page_index * slot_count + slot_index
    sources = jnp.arange(device_count, dtype=jnp.int32)
    source_page = sources // slot_count
    source_slot = sources % slot_count
    source_grid = source_slot - firsts[source_page]
    source_thumb = source_slot == thumbs[source_page]
    source_live = (source_grid >= 0) & (source_grid < tile_totals[source_page]) | source_thumb
    source_start = (
        starts[source_page]
        + texts[source_page]
        + jnp.where(source_thumb, tile_totals[source_page], source_grid) * SHUF
    )
    first_row = (source_start + (own_rank - source_start) % device_count) // device_count
    shard_rows = SHUF + TXTMAX // slot_count
    targets = first_row[None, :] + jnp.arange(per_peer, dtype=jnp.int32)[:, None]
    targets = jnp.where(source_live[None, :], targets, shard_rows)
    placed = jnp.zeros((shard_rows, 4 * HH), jnp.bfloat16)
    return placed.at[targets.reshape(-1)].set(arrived.reshape(-1, 4 * HH), mode="drop")


def solution(mesh):
    placed = (
        P("dp", "tile", None, None),
        P("dp", "tile", None, None),
        P("dp", "tile", None, None),
        P(),
    )
    return jax.shard_map(
        body, mesh=mesh, in_specs=placed, out_specs=P(("dp", "tile"), None), check_vma=False
    )
```

```python
import jax
import jax.numpy as jnp
from jax import lax
from jax.experimental import pallas as pl
from jax.experimental.pallas import tpu as pltpu
from jax.sharding import PartitionSpec as P

HEADS = 13
HD = 128
GRID = 32
TXTMAX = 256
HH = 1664
TOK = 1024
SHUF = 256
HEAD_CHUNKS = ((0, 4), (4, 8), (8, 13))


def passed_along(value, axis, steps):
    count = lax.axis_size(axis)
    initial, last = (max(0, -steps), min(count, count - steps))
    return lax.ppermute(value, axis, [(source, source + steps) for source in range(initial, last)])


def block_terms(query, k_ref, v_ref):
    scores = lax.dot_general(
        query, k_ref[...], (((1,), (1,)), ((), ())), preferred_element_type=jnp.float32
    ) * HD ** (-0.5)
    largest = jnp.max(scores, axis=1, keepdims=True)
    weights = jnp.exp(scores - largest).astype(jnp.bfloat16)
    ones = jnp.ones((TOK, HD), jnp.bfloat16)
    both = jnp.dot(
        weights, jnp.concatenate([v_ref[...], ones], axis=1), preferred_element_type=jnp.float32
    )
    return both[:, :HD], largest, both[:, HD : HD + 1]


def merge_block(flag, query, k_ref, v_ref, acc_ref, top_ref, sum_ref):
    @pl.when(flag != 0)
    def _():
        numerator, largest, totals = block_terms(query, k_ref, v_ref)
        old_top = top_ref[...]
        new_top = jnp.maximum(old_top, largest)
        keep = jnp.exp(old_top - new_top)
        take = jnp.exp(largest - new_top)
        acc_ref[...] = acc_ref[...] * keep + numerator * take
        sum_ref[...] = sum_ref[...] * keep + totals * take
        top_ref[...] = new_top


def near_kernel(flags_ref, q_ref, k0, v0, k1, v1, k2, v2, acc_prev, top_prev, sum_prev, acc_ref, top_ref, sum_ref):
    query = q_ref[...]
    numerator, largest, totals = block_terms(query, k0, v0)
    acc_ref[...] = numerator
    top_ref[0] = largest
    sum_ref[0] = totals
    merge_block(flags_ref[0], query, k1, v1, acc_ref, top_ref.at[0], sum_ref.at[0])
    merge_block(flags_ref[1], query, k2, v2, acc_ref, top_ref.at[0], sum_ref.at[0])


def thumb_kernel(flags_ref, q_ref, k3, v3, acc_in, top_in, sum_in, o_ref, acc_ref, top_ref, sum_ref):
    acc_ref[...] = acc_in[...]
    top_ref[...] = top_in[0]
    sum_ref[...] = sum_in[0]
    merge_block(flags_ref[2], q_ref[...], k3, v3, acc_ref, top_ref, sum_ref)
    o_ref[...] = (acc_ref[...] / sum_ref[...]).astype(o_ref.dtype)


def attend_near(flags, query_cols, blocks, first_head, head_count, state):
    q_spec = pl.BlockSpec((TOK, HD), lambda h, flags: (0, h))
    v_spec = pl.BlockSpec((TOK, HD), lambda h, flags: (0, head_count + h))
    acc_spec = pl.BlockSpec((TOK, HD), lambda h, flags: (0, first_head + h))
    stat_spec = pl.BlockSpec((1, TOK, 1), lambda h, flags: (first_head + h, 0, 0))
    held = pl.BlockSpec(memory_space=pl.ANY)
    operands = []
    for both in blocks:
        operands += [both, both]
    count = 1 + len(operands)
    return pl.pallas_call(
        near_kernel,
        grid_spec=pltpu.PrefetchScalarGridSpec(
            num_scalar_prefetch=1,
            grid=(head_count,),
            in_specs=[q_spec] + [q_spec, v_spec] * len(blocks) + [held] * 3,
            out_specs=[acc_spec, stat_spec, stat_spec],
        ),
        out_shape=[
            jax.ShapeDtypeStruct((TOK, HH), jnp.float32),
            jax.ShapeDtypeStruct((HEADS, TOK, 1), jnp.float32),
            jax.ShapeDtypeStruct((HEADS, TOK, 1), jnp.float32),
        ],
        input_output_aliases={count + 1: 0, count + 2: 1, count + 3: 2},
    )(flags, query_cols, *operands, *state)


def attend_thumb(flags, query_tile, thumb_keys, thumb_values, acc, top, totals):
    q_spec = pl.BlockSpec((TOK, HD), lambda h, flags: (0, h))
    stat_spec = pl.BlockSpec((1, TOK, 1), lambda h, flags: (h, 0, 0))
    return pl.pallas_call(
        thumb_kernel,
        grid_spec=pltpu.PrefetchScalarGridSpec(
            num_scalar_prefetch=1,
            grid=(HEADS,),
            in_specs=[q_spec, q_spec, q_spec, q_spec, stat_spec, stat_spec],
            out_specs=q_spec,
            scratch_shapes=[
                pltpu.VMEM((TOK, HD), jnp.float32),
                pltpu.VMEM((TOK, 1), jnp.float32),
                pltpu.VMEM((TOK, 1), jnp.float32),
            ],
        ),
        out_shape=jax.ShapeDtypeStruct((TOK, HH), jnp.bfloat16),
    )(flags, query_tile, thumb_keys, thumb_values, acc, top, totals)


def pixel_shuffle(attended):
    half_grid = GRID // 2
    width = attended.shape[-1]
    return (
        attended.reshape(half_grid, 2, half_grid, 2, width)
        .transpose(0, 2, 1, 3, 4)
        .reshape(half_grid * half_grid, 4 * width)
    )


def page_layout(page_info):
    columns = page_info[:, 0]
    tile_totals = columns * page_info[:, 1]
    thumbs = page_info[:, 2]
    texts = page_info[:, 3]
    firsts = page_info[:, 4]
    lengths = texts + (tile_totals + 1) * SHUF
    starts = jnp.cumsum(lengths) - lengths
    return (columns, tile_totals, thumbs, texts, starts, firsts)


def body(queries, keys, values, page_info):
    query_tile = queries.reshape(TOK, HH)
    key_tile = keys.reshape(TOK, HH)
    value_tile = values.reshape(TOK, HH)
    slot_count = lax.axis_size("tile")
    page_count = lax.axis_size("dp")
    device_count = page_count * slot_count
    page_index = lax.axis_index("dp")
    slot_index = lax.axis_index("tile")
    columns, tile_totals, thumbs, texts, starts, firsts = page_layout(page_info)
    grid_width = columns[page_index]
    tile_total = tile_totals[page_index]
    thumb_slot = thumbs[page_index]
    grid_pos = slot_index - firsts[page_index]
    is_tile = (grid_pos >= 0) & (grid_pos < tile_total)
    has_left = is_tile & (grid_pos % grid_width > 0)
    has_right = is_tile & (grid_pos % grid_width < grid_width - 1)
    flags = jnp.stack([has_left, has_right, is_tile]).astype(jnp.int32)
    is_thumb = slot_index == thumb_slot
    is_live = is_tile | is_thumb
    row_start = (
        starts[page_index] + texts[page_index] + jnp.where(is_thumb, tile_total, grid_pos) * SHUF
    )
    per_peer = SHUF // device_count
    query_tile = jnp.roll(
        pixel_shuffle(query_tile).reshape(per_peer, device_count, 4 * HH),
        row_start % device_count,
        axis=1,
    ).reshape(TOK, HH)

    mine = slot_index == thumb_slot
    thumb_keys = lax.psum(jnp.where(mine, key_tile, jnp.zeros_like(key_tile)), "tile")
    thumb_values = lax.psum(jnp.where(mine, value_tile, jnp.zeros_like(value_tile)), "tile")
    state = (
        jnp.zeros((TOK, HH), jnp.float32),
        jnp.zeros((HEADS, TOK, 1), jnp.float32),
        jnp.zeros((HEADS, TOK, 1), jnp.float32),
    )
    arrived_last = None
    state_before = None
    for first_head, end_head in HEAD_CHUNKS:
        head_count = end_head - first_head
        cols = slice(first_head * HD, end_head * HD)
        own = jnp.concatenate([key_tile[:, cols], value_tile[:, cols]], axis=1)
        if arrived_last is not None:
            arrived_last, state_before, own = lax.optimization_barrier((arrived_last, state_before, own))
        left = passed_along(own, "tile", 1)
        right = passed_along(own, "tile", -1)
        arrived_last = (left, right)
        state_before = state
        state = attend_near(
            flags, query_tile[:, cols], (own, left, right), first_head, head_count, state
        )
    attended = attend_thumb(flags, query_tile, thumb_keys, thumb_values, *state)
    arranged = attended.reshape(per_peer, device_count, 4 * HH)
    arranged = jnp.where(is_live, arranged, jnp.zeros_like(arranged))
    arrived = lax.all_to_all(arranged, ("dp", "tile"), split_axis=1, concat_axis=1, tiled=True)
    own_rank = page_index * slot_count + slot_index
    sources = jnp.arange(device_count, dtype=jnp.int32)
    source_page = sources // slot_count
    source_slot = sources % slot_count
    source_grid = source_slot - firsts[source_page]
    source_thumb = source_slot == thumbs[source_page]
    source_live = (source_grid >= 0) & (source_grid < tile_totals[source_page]) | source_thumb
    source_start = (
        starts[source_page]
        + texts[source_page]
        + jnp.where(source_thumb, tile_totals[source_page], source_grid) * SHUF
    )
    first_row = (source_start + (own_rank - source_start) % device_count) // device_count
    shard_rows = SHUF + TXTMAX // slot_count
    targets = first_row[None, :] + jnp.arange(per_peer, dtype=jnp.int32)[:, None]
    targets = jnp.where(source_live[None, :], targets, shard_rows)
    placed = jnp.zeros((shard_rows, 4 * HH), jnp.bfloat16)
    return placed.at[targets.reshape(-1)].set(arrived.reshape(-1, 4 * HH), mode="drop")


def solution(mesh):
    placed = (
        P("dp", "tile", None, None),
        P("dp", "tile", None, None),
        P("dp", "tile", None, None),
        P(),
    )
    return jax.shard_map(
        body, mesh=mesh, in_specs=placed, out_specs=P(("dp", "tile"), None), check_vma=False
    )
```

```python
import jax
import jax.numpy as jnp
from jax import lax
from jax.experimental import pallas as pl
from jax.experimental.pallas import tpu as pltpu
from jax.sharding import PartitionSpec as P

HEADS = 13
HD = 128
GRID = 32
TXTMAX = 256
HH = 1664
TOK = 1024
SHUF = 256
HEAD_CHUNKS = ((0, 4), (4, 8), (8, 11), (11, 13))


def passed_along(value, axis, steps):
    count = lax.axis_size(axis)
    initial, last = (max(0, -steps), min(count, count - steps))
    return lax.ppermute(value, axis, [(source, source + steps) for source in range(initial, last)])


def block_terms(query, k_ref, v_ref):
    scores = lax.dot_general(
        query, k_ref[...], (((1,), (1,)), ((), ())), preferred_element_type=jnp.float32
    ) * HD ** (-0.5)
    largest = jnp.max(scores, axis=1, keepdims=True)
    weights = jnp.exp(scores - largest).astype(jnp.bfloat16)
    ones = jnp.ones((TOK, HD), jnp.bfloat16)
    both = jnp.dot(
        weights, jnp.concatenate([v_ref[...], ones], axis=1), preferred_element_type=jnp.float32
    )
    return both[:, :HD], largest, both[:, HD : HD + 1]


def merge_block(flag, query, k_ref, v_ref, acc_ref, top_ref, sum_ref):
    @pl.when(flag != 0)
    def _():
        numerator, largest, totals = block_terms(query, k_ref, v_ref)
        old_top = top_ref[...]
        new_top = jnp.maximum(old_top, largest)
        keep = jnp.exp(old_top - new_top)
        take = jnp.exp(largest - new_top)
        acc_ref[...] = acc_ref[...] * keep + numerator * take
        sum_ref[...] = sum_ref[...] * keep + totals * take
        top_ref[...] = new_top


def near_kernel(flags_ref, q_ref, k0, v0, k1, v1, k2, v2, acc_prev, top_prev, sum_prev, acc_ref, top_ref, sum_ref):
    query = q_ref[...]
    numerator, largest, totals = block_terms(query, k0, v0)
    acc_ref[...] = numerator
    top_ref[0] = largest
    sum_ref[0] = totals
    merge_block(flags_ref[0], query, k1, v1, acc_ref, top_ref.at[0], sum_ref.at[0])
    merge_block(flags_ref[1], query, k2, v2, acc_ref, top_ref.at[0], sum_ref.at[0])


def thumb_kernel(flags_ref, q_ref, k3, v3, acc_in, top_in, sum_in, o_ref, acc_ref, top_ref, sum_ref):
    acc_ref[...] = acc_in[...]
    top_ref[...] = top_in[0]
    sum_ref[...] = sum_in[0]
    merge_block(flags_ref[2], q_ref[...], k3, v3, acc_ref, top_ref, sum_ref)
    o_ref[...] = (acc_ref[...] / sum_ref[...]).astype(o_ref.dtype)


def attend_near(flags, query_cols, blocks, first_head, head_count, state):
    q_spec = pl.BlockSpec((TOK, HD), lambda h, flags: (0, h))
    v_spec = pl.BlockSpec((TOK, HD), lambda h, flags: (0, head_count + h))
    acc_spec = pl.BlockSpec((TOK, HD), lambda h, flags: (0, first_head + h))
    stat_spec = pl.BlockSpec((1, TOK, 1), lambda h, flags: (first_head + h, 0, 0))
    held = pl.BlockSpec(memory_space=pl.ANY)
    operands = []
    for both in blocks:
        operands += [both, both]
    count = 1 + len(operands)
    return pl.pallas_call(
        near_kernel,
        grid_spec=pltpu.PrefetchScalarGridSpec(
            num_scalar_prefetch=1,
            grid=(head_count,),
            in_specs=[q_spec] + [q_spec, v_spec] * len(blocks) + [held] * 3,
            out_specs=[acc_spec, stat_spec, stat_spec],
        ),
        out_shape=[
            jax.ShapeDtypeStruct((TOK, HH), jnp.float32),
            jax.ShapeDtypeStruct((HEADS, TOK, 1), jnp.float32),
            jax.ShapeDtypeStruct((HEADS, TOK, 1), jnp.float32),
        ],
        input_output_aliases={count + 1: 0, count + 2: 1, count + 3: 2},
    )(flags, query_cols, *operands, *state)


def attend_thumb(flags, query_tile, thumb_keys, thumb_values, acc, top, totals):
    q_spec = pl.BlockSpec((TOK, HD), lambda h, flags: (0, h))
    stat_spec = pl.BlockSpec((1, TOK, 1), lambda h, flags: (h, 0, 0))
    return pl.pallas_call(
        thumb_kernel,
        grid_spec=pltpu.PrefetchScalarGridSpec(
            num_scalar_prefetch=1,
            grid=(HEADS,),
            in_specs=[q_spec, q_spec, q_spec, q_spec, stat_spec, stat_spec],
            out_specs=q_spec,
            scratch_shapes=[
                pltpu.VMEM((TOK, HD), jnp.float32),
                pltpu.VMEM((TOK, 1), jnp.float32),
                pltpu.VMEM((TOK, 1), jnp.float32),
            ],
        ),
        out_shape=jax.ShapeDtypeStruct((TOK, HH), jnp.bfloat16),
    )(flags, query_tile, thumb_keys, thumb_values, acc, top, totals)


def pixel_shuffle(attended):
    half_grid = GRID // 2
    width = attended.shape[-1]
    return (
        attended.reshape(half_grid, 2, half_grid, 2, width)
        .transpose(0, 2, 1, 3, 4)
        .reshape(half_grid * half_grid, 4 * width)
    )


def page_layout(page_info):
    columns = page_info[:, 0]
    tile_totals = columns * page_info[:, 1]
    thumbs = page_info[:, 2]
    texts = page_info[:, 3]
    firsts = page_info[:, 4]
    lengths = texts + (tile_totals + 1) * SHUF
    starts = jnp.cumsum(lengths) - lengths
    return (columns, tile_totals, thumbs, texts, starts, firsts)


def body(queries, keys, values, page_info):
    query_tile = queries.reshape(TOK, HH)
    key_tile = keys.reshape(TOK, HH)
    value_tile = values.reshape(TOK, HH)
    slot_count = lax.axis_size("tile")
    page_count = lax.axis_size("dp")
    device_count = page_count * slot_count
    page_index = lax.axis_index("dp")
    slot_index = lax.axis_index("tile")
    columns, tile_totals, thumbs, texts, starts, firsts = page_layout(page_info)
    grid_width = columns[page_index]
    tile_total = tile_totals[page_index]
    thumb_slot = thumbs[page_index]
    grid_pos = slot_index - firsts[page_index]
    is_tile = (grid_pos >= 0) & (grid_pos < tile_total)
    has_left = is_tile & (grid_pos % grid_width > 0)
    has_right = is_tile & (grid_pos % grid_width < grid_width - 1)
    flags = jnp.stack([has_left, has_right, is_tile]).astype(jnp.int32)
    is_thumb = slot_index == thumb_slot
    is_live = is_tile | is_thumb
    row_start = (
        starts[page_index] + texts[page_index] + jnp.where(is_thumb, tile_total, grid_pos) * SHUF
    )
    per_peer = SHUF // device_count
    query_tile = jnp.roll(
        pixel_shuffle(query_tile).reshape(per_peer, device_count, 4 * HH),
        row_start % device_count,
        axis=1,
    ).reshape(TOK, HH)

    mine = slot_index == thumb_slot
    thumb_keys = lax.psum(jnp.where(mine, key_tile, jnp.zeros_like(key_tile)), "tile")
    thumb_values = lax.psum(jnp.where(mine, value_tile, jnp.zeros_like(value_tile)), "tile")
    state = (
        jnp.zeros((TOK, HH), jnp.float32),
        jnp.zeros((HEADS, TOK, 1), jnp.float32),
        jnp.zeros((HEADS, TOK, 1), jnp.float32),
    )
    arrived_last = None
    state_before = None
    for first_head, end_head in HEAD_CHUNKS:
        head_count = end_head - first_head
        cols = slice(first_head * HD, end_head * HD)
        own = jnp.concatenate([key_tile[:, cols], value_tile[:, cols]], axis=1)
        if arrived_last is not None:
            arrived_last, state_before, own = lax.optimization_barrier((arrived_last, state_before, own))
        left = passed_along(own, "tile", 1)
        right = passed_along(own, "tile", -1)
        arrived_last = (left, right)
        state_before = state
        state = attend_near(
            flags, query_tile[:, cols], (own, left, right), first_head, head_count, state
        )
    attended = attend_thumb(flags, query_tile, thumb_keys, thumb_values, *state)
    arranged = attended.reshape(per_peer, device_count, 4 * HH)
    arranged = jnp.where(is_live, arranged, jnp.zeros_like(arranged))
    arrived = lax.all_to_all(arranged, ("dp", "tile"), split_axis=1, concat_axis=1, tiled=True)
    own_rank = page_index * slot_count + slot_index
    sources = jnp.arange(device_count, dtype=jnp.int32)
    source_page = sources // slot_count
    source_slot = sources % slot_count
    source_grid = source_slot - firsts[source_page]
    source_thumb = source_slot == thumbs[source_page]
    source_live = (source_grid >= 0) & (source_grid < tile_totals[source_page]) | source_thumb
    source_start = (
        starts[source_page]
        + texts[source_page]
        + jnp.where(source_thumb, tile_totals[source_page], source_grid) * SHUF
    )
    first_row = (source_start + (own_rank - source_start) % device_count) // device_count
    shard_rows = SHUF + TXTMAX // slot_count
    targets = first_row[None, :] + jnp.arange(per_peer, dtype=jnp.int32)[:, None]
    targets = jnp.where(source_live[None, :], targets, shard_rows)
    placed = jnp.zeros((shard_rows, 4 * HH), jnp.bfloat16)
    return placed.at[targets.reshape(-1)].set(arrived.reshape(-1, 4 * HH), mode="drop")


def solution(mesh):
    placed = (
        P("dp", "tile", None, None),
        P("dp", "tile", None, None),
        P("dp", "tile", None, None),
        P(),
    )
    return jax.shard_map(
        body, mesh=mesh, in_specs=placed, out_specs=P(("dp", "tile"), None), check_vma=False
    )
```

```python
import jax
import jax.numpy as jnp
from jax import lax
from jax.experimental import pallas as pl
from jax.experimental.pallas import tpu as pltpu
from jax.sharding import PartitionSpec as P

HEADS = 13
HD = 128
GRID = 32
TXTMAX = 256
HH = 1664
TOK = 1024
SHUF = 256
HEAD_CHUNKS = ((0, 4), (4, 8), (8, 11), (11, 13))


def passed_along(value, axis, steps):
    count = lax.axis_size(axis)
    initial, last = (max(0, -steps), min(count, count - steps))
    return lax.ppermute(value, axis, [(source, source + steps) for source in range(initial, last)])


def block_terms(query, k_ref, v_ref):
    scores = lax.dot_general(
        query, k_ref[...], (((1,), (1,)), ((), ())), preferred_element_type=jnp.float32
    ) * HD ** (-0.5)
    largest = jnp.max(scores, axis=1, keepdims=True)
    weights = jnp.exp(scores - largest).astype(jnp.bfloat16)
    ones = jnp.ones((TOK, HD), jnp.bfloat16)
    both = jnp.dot(
        weights, jnp.concatenate([v_ref[...], ones], axis=1), preferred_element_type=jnp.float32
    )
    return both[:, :HD], largest, both[:, HD : HD + 1]


def merge_block(flag, query, k_ref, v_ref, acc_ref, top_ref, sum_ref):
    @pl.when(flag != 0)
    def _():
        numerator, largest, totals = block_terms(query, k_ref, v_ref)
        old_top = top_ref[...]
        new_top = jnp.maximum(old_top, largest)
        keep = jnp.exp(old_top - new_top)
        take = jnp.exp(largest - new_top)
        acc_ref[...] = acc_ref[...] * keep + numerator * take
        sum_ref[...] = sum_ref[...] * keep + totals * take
        top_ref[...] = new_top


def near_kernel(flags_ref, q_ref, k0, v0, k1, v1, k2, v2, acc_prev, top_prev, sum_prev, acc_ref, top_ref, sum_ref):
    query = q_ref[...]
    numerator, largest, totals = block_terms(query, k0, v0)
    acc_ref[...] = numerator
    top_ref[0] = largest
    sum_ref[0] = totals
    merge_block(flags_ref[0], query, k1, v1, acc_ref, top_ref.at[0], sum_ref.at[0])
    merge_block(flags_ref[1], query, k2, v2, acc_ref, top_ref.at[0], sum_ref.at[0])


def thumb_kernel(flags_ref, q_ref, k3, v3, acc_in, top_in, sum_in, o_ref, acc_ref, top_ref, sum_ref):
    acc_ref[...] = acc_in[...]
    top_ref[...] = top_in[0]
    sum_ref[...] = sum_in[0]
    merge_block(flags_ref[2], q_ref[...], k3, v3, acc_ref, top_ref, sum_ref)
    o_ref[...] = (acc_ref[...] / sum_ref[...]).astype(o_ref.dtype)


def attend_near(flags, query_cols, blocks, first_head, head_count, state):
    q_spec = pl.BlockSpec((TOK, HD), lambda h, flags: (0, h))
    v_spec = pl.BlockSpec((TOK, HD), lambda h, flags: (0, head_count + h))
    acc_spec = pl.BlockSpec((TOK, HD), lambda h, flags: (0, first_head + h))
    stat_spec = pl.BlockSpec((1, TOK, 1), lambda h, flags: (first_head + h, 0, 0))
    held = pl.BlockSpec(memory_space=pl.ANY)
    operands = []
    for both in blocks:
        operands += [both, both]
    count = 1 + len(operands)
    return pl.pallas_call(
        near_kernel,
        grid_spec=pltpu.PrefetchScalarGridSpec(
            num_scalar_prefetch=1,
            grid=(head_count,),
            in_specs=[q_spec] + [q_spec, v_spec] * len(blocks) + [held] * 3,
            out_specs=[acc_spec, stat_spec, stat_spec],
        ),
        out_shape=[
            jax.ShapeDtypeStruct((TOK, HH), jnp.float32),
            jax.ShapeDtypeStruct((HEADS, TOK, 1), jnp.float32),
            jax.ShapeDtypeStruct((HEADS, TOK, 1), jnp.float32),
        ],
        input_output_aliases={count + 1: 0, count + 2: 1, count + 3: 2},
    )(flags, query_cols, *operands, *state)


def attend_thumb(flags, query_tile, thumb_keys, thumb_values, acc, top, totals):
    q_spec = pl.BlockSpec((TOK, HD), lambda h, flags: (0, h))
    stat_spec = pl.BlockSpec((1, TOK, 1), lambda h, flags: (h, 0, 0))
    return pl.pallas_call(
        thumb_kernel,
        grid_spec=pltpu.PrefetchScalarGridSpec(
            num_scalar_prefetch=1,
            grid=(HEADS,),
            in_specs=[q_spec, q_spec, q_spec, q_spec, stat_spec, stat_spec],
            out_specs=q_spec,
            scratch_shapes=[
                pltpu.VMEM((TOK, HD), jnp.float32),
                pltpu.VMEM((TOK, 1), jnp.float32),
                pltpu.VMEM((TOK, 1), jnp.float32),
            ],
        ),
        out_shape=jax.ShapeDtypeStruct((TOK, HH), jnp.bfloat16),
    )(flags, query_tile, thumb_keys, thumb_values, acc, top, totals)


def pixel_shuffle(attended):
    half_grid = GRID // 2
    width = attended.shape[-1]
    return (
        attended.reshape(half_grid, 2, half_grid, 2, width)
        .transpose(0, 2, 1, 3, 4)
        .reshape(half_grid * half_grid, 4 * width)
    )


def page_layout(page_info):
    columns = page_info[:, 0]
    tile_totals = columns * page_info[:, 1]
    thumbs = page_info[:, 2]
    texts = page_info[:, 3]
    firsts = page_info[:, 4]
    lengths = texts + (tile_totals + 1) * SHUF
    starts = jnp.cumsum(lengths) - lengths
    return (columns, tile_totals, thumbs, texts, starts, firsts)


def body(queries, keys, values, page_info):
    query_tile = queries.reshape(TOK, HH)
    key_tile = keys.reshape(TOK, HH)
    value_tile = values.reshape(TOK, HH)
    slot_count = lax.axis_size("tile")
    page_count = lax.axis_size("dp")
    device_count = page_count * slot_count
    page_index = lax.axis_index("dp")
    slot_index = lax.axis_index("tile")
    columns, tile_totals, thumbs, texts, starts, firsts = page_layout(page_info)
    grid_width = columns[page_index]
    tile_total = tile_totals[page_index]
    thumb_slot = thumbs[page_index]
    grid_pos = slot_index - firsts[page_index]
    is_tile = (grid_pos >= 0) & (grid_pos < tile_total)
    has_left = is_tile & (grid_pos % grid_width > 0)
    has_right = is_tile & (grid_pos % grid_width < grid_width - 1)
    flags = jnp.stack([has_left, has_right, is_tile]).astype(jnp.int32)
    is_thumb = slot_index == thumb_slot
    is_live = is_tile | is_thumb
    row_start = (
        starts[page_index] + texts[page_index] + jnp.where(is_thumb, tile_total, grid_pos) * SHUF
    )
    per_peer = SHUF // device_count
    query_tile = (
        jnp.roll(
            pixel_shuffle(query_tile).reshape(per_peer, device_count, 4 * HH),
            row_start % device_count,
            axis=1,
        )
        .transpose(1, 0, 2)
        .reshape(TOK, HH)
    )

    mine = slot_index == thumb_slot
    thumb_keys = lax.psum(jnp.where(mine, key_tile, jnp.zeros_like(key_tile)), "tile")
    thumb_values = lax.psum(jnp.where(mine, value_tile, jnp.zeros_like(value_tile)), "tile")
    state = (
        jnp.zeros((TOK, HH), jnp.float32),
        jnp.zeros((HEADS, TOK, 1), jnp.float32),
        jnp.zeros((HEADS, TOK, 1), jnp.float32),
    )
    arrived_last = None
    state_before = None
    for first_head, end_head in HEAD_CHUNKS:
        head_count = end_head - first_head
        cols = slice(first_head * HD, end_head * HD)
        own = jnp.concatenate([key_tile[:, cols], value_tile[:, cols]], axis=1)
        if arrived_last is not None:
            arrived_last, state_before, own = lax.optimization_barrier((arrived_last, state_before, own))
        left = passed_along(own, "tile", 1)
        right = passed_along(own, "tile", -1)
        arrived_last = (left, right)
        state_before = state
        state = attend_near(
            flags, query_tile[:, cols], (own, left, right), first_head, head_count, state
        )
    attended = attend_thumb(flags, query_tile, thumb_keys, thumb_values, *state)
    arranged = attended.reshape(device_count, per_peer, 4 * HH)
    arrived = lax.all_to_all(arranged, ("dp", "tile"), split_axis=0, concat_axis=0, tiled=True)
    own_rank = page_index * slot_count + slot_index
    sources = jnp.arange(device_count, dtype=jnp.int32)
    source_page = sources // slot_count
    source_slot = sources % slot_count
    source_grid = source_slot - firsts[source_page]
    source_thumb = source_slot == thumbs[source_page]
    source_live = (source_grid >= 0) & (source_grid < tile_totals[source_page]) | source_thumb
    source_start = (
        starts[source_page]
        + texts[source_page]
        + jnp.where(source_thumb, tile_totals[source_page], source_grid) * SHUF
    )
    first_row = (source_start + (own_rank - source_start) % device_count) // device_count
    shard_rows = SHUF + TXTMAX // slot_count
    targets = first_row[:, None] + jnp.arange(per_peer, dtype=jnp.int32)[None, :]
    targets = jnp.where(source_live[:, None], targets, shard_rows)
    placed = jnp.zeros((shard_rows, 4 * HH), jnp.bfloat16)
    return placed.at[targets.reshape(-1)].set(arrived.reshape(-1, 4 * HH), mode="drop")


def solution(mesh):
    placed = (
        P("dp", "tile", None, None),
        P("dp", "tile", None, None),
        P("dp", "tile", None, None),
        P(),
    )
    return jax.shard_map(
        body, mesh=mesh, in_specs=placed, out_specs=P(("dp", "tile"), None), check_vma=False
    )
```

```python
import jax
import jax.numpy as jnp
from jax import lax
from jax.experimental import pallas as pl
from jax.experimental.pallas import tpu as pltpu
from jax.sharding import PartitionSpec as P

HEADS = 13
HD = 128
GRID = 32
TXTMAX = 256
HH = 1664
TOK = 1024
SHUF = 256
HEAD_CHUNKS = ((0, 4), (4, 8), (8, 11), (11, 13))


def passed_along(value, axis, steps):
    count = lax.axis_size(axis)
    initial, last = (max(0, -steps), min(count, count - steps))
    return lax.ppermute(value, axis, [(source, source + steps) for source in range(initial, last)])


def block_terms(query, k_ref, v_ref):
    scores = lax.dot_general(
        query, k_ref[...], (((1,), (1,)), ((), ())), preferred_element_type=jnp.float32
    ) * HD ** (-0.5)
    largest = jnp.max(scores, axis=1, keepdims=True)
    weights = jnp.exp(scores - largest).astype(jnp.bfloat16)
    ones = jnp.ones((TOK, HD), jnp.bfloat16)
    both = jnp.dot(
        weights, jnp.concatenate([v_ref[...], ones], axis=1), preferred_element_type=jnp.float32
    )
    return both[:, :HD], largest, both[:, HD : HD + 1]


def merge_block(flag, query, k_ref, v_ref, acc_ref, top_ref, sum_ref):
    @pl.when(flag != 0)
    def _():
        numerator, largest, totals = block_terms(query, k_ref, v_ref)
        old_top = top_ref[...]
        new_top = jnp.maximum(old_top, largest)
        keep = jnp.exp(old_top - new_top)
        take = jnp.exp(largest - new_top)
        acc_ref[...] = acc_ref[...] * keep + numerator * take
        sum_ref[...] = sum_ref[...] * keep + totals * take
        top_ref[...] = new_top


def near_kernel(flags_ref, q_ref, k0, v0, k1, v1, k2, v2, acc_prev, top_prev, sum_prev, acc_ref, top_ref, sum_ref):
    query = q_ref[...]
    numerator, largest, totals = block_terms(query, k0, v0)
    acc_ref[...] = numerator
    top_ref[0] = largest
    sum_ref[0] = totals
    merge_block(flags_ref[0], query, k1, v1, acc_ref, top_ref.at[0], sum_ref.at[0])
    merge_block(flags_ref[1], query, k2, v2, acc_ref, top_ref.at[0], sum_ref.at[0])


def thumb_kernel(flags_ref, q_ref, k3, v3, acc_in, top_in, sum_in, o_ref, acc_ref, top_ref, sum_ref):
    acc_ref[...] = acc_in[...]
    top_ref[...] = top_in[0]
    sum_ref[...] = sum_in[0]
    merge_block(flags_ref[2], q_ref[...], k3, v3, acc_ref, top_ref, sum_ref)
    attended = (acc_ref[...] / sum_ref[...]).astype(o_ref.dtype)
    head = pl.program_id(0)
    for patch in range(4):
        column = pl.multiple_of(patch * HH + head * HD, HD)
        o_ref[:, pl.ds(column, HD)] = attended[patch * SHUF : (patch + 1) * SHUF]


def attend_near(flags, query_cols, blocks, first_head, head_count, state):
    q_spec = pl.BlockSpec((TOK, HD), lambda h, flags: (0, h))
    v_spec = pl.BlockSpec((TOK, HD), lambda h, flags: (0, head_count + h))
    acc_spec = pl.BlockSpec((TOK, HD), lambda h, flags: (0, first_head + h))
    stat_spec = pl.BlockSpec((1, TOK, 1), lambda h, flags: (first_head + h, 0, 0))
    held = pl.BlockSpec(memory_space=pl.ANY)
    operands = []
    for both in blocks:
        operands += [both, both]
    count = 1 + len(operands)
    return pl.pallas_call(
        near_kernel,
        grid_spec=pltpu.PrefetchScalarGridSpec(
            num_scalar_prefetch=1,
            grid=(head_count,),
            in_specs=[q_spec] + [q_spec, v_spec] * len(blocks) + [held] * 3,
            out_specs=[acc_spec, stat_spec, stat_spec],
        ),
        out_shape=[
            jax.ShapeDtypeStruct((TOK, HH), jnp.float32),
            jax.ShapeDtypeStruct((HEADS, TOK, 1), jnp.float32),
            jax.ShapeDtypeStruct((HEADS, TOK, 1), jnp.float32),
        ],
        input_output_aliases={count + 1: 0, count + 2: 1, count + 3: 2},
    )(flags, query_cols, *operands, *state)


def attend_thumb(flags, query_tile, thumb_keys, thumb_values, acc, top, totals):
    q_spec = pl.BlockSpec((TOK, HD), lambda h, flags: (0, h))
    stat_spec = pl.BlockSpec((1, TOK, 1), lambda h, flags: (h, 0, 0))
    return pl.pallas_call(
        thumb_kernel,
        grid_spec=pltpu.PrefetchScalarGridSpec(
            num_scalar_prefetch=1,
            grid=(HEADS,),
            in_specs=[q_spec, q_spec, q_spec, q_spec, stat_spec, stat_spec],
            out_specs=pl.BlockSpec((SHUF, 4 * HH), lambda h, flags: (0, 0)),
            scratch_shapes=[
                pltpu.VMEM((TOK, HD), jnp.float32),
                pltpu.VMEM((TOK, 1), jnp.float32),
                pltpu.VMEM((TOK, 1), jnp.float32),
            ],
        ),
        out_shape=jax.ShapeDtypeStruct((SHUF, 4 * HH), jnp.bfloat16),
    )(flags, query_tile, thumb_keys, thumb_values, acc, top, totals)


def pixel_shuffle(attended):
    half_grid = GRID // 2
    width = attended.shape[-1]
    return (
        attended.reshape(half_grid, 2, half_grid, 2, width)
        .transpose(0, 2, 1, 3, 4)
        .reshape(half_grid * half_grid, 4 * width)
    )


def page_layout(page_info):
    columns = page_info[:, 0]
    tile_totals = columns * page_info[:, 1]
    thumbs = page_info[:, 2]
    texts = page_info[:, 3]
    firsts = page_info[:, 4]
    lengths = texts + (tile_totals + 1) * SHUF
    starts = jnp.cumsum(lengths) - lengths
    return (columns, tile_totals, thumbs, texts, starts, firsts)


def body(queries, keys, values, page_info):
    query_tile = queries.reshape(TOK, HH)
    key_tile = keys.reshape(TOK, HH)
    value_tile = values.reshape(TOK, HH)
    slot_count = lax.axis_size("tile")
    page_count = lax.axis_size("dp")
    device_count = page_count * slot_count
    page_index = lax.axis_index("dp")
    slot_index = lax.axis_index("tile")
    columns, tile_totals, thumbs, texts, starts, firsts = page_layout(page_info)
    grid_width = columns[page_index]
    tile_total = tile_totals[page_index]
    thumb_slot = thumbs[page_index]
    grid_pos = slot_index - firsts[page_index]
    is_tile = (grid_pos >= 0) & (grid_pos < tile_total)
    has_left = is_tile & (grid_pos % grid_width > 0)
    has_right = is_tile & (grid_pos % grid_width < grid_width - 1)
    flags = jnp.stack([has_left, has_right, is_tile]).astype(jnp.int32)
    is_thumb = slot_index == thumb_slot
    is_live = is_tile | is_thumb
    row_start = (
        starts[page_index] + texts[page_index] + jnp.where(is_thumb, tile_total, grid_pos) * SHUF
    )
    per_peer = SHUF // device_count
    query_tile = (
        jnp.roll(
            pixel_shuffle(query_tile).reshape(per_peer, device_count, 4 * HH),
            row_start % device_count,
            axis=1,
        )
        .transpose(1, 0, 2)
        .reshape(SHUF, 4, HH)
        .transpose(1, 0, 2)
        .reshape(TOK, HH)
    )

    mine = slot_index == thumb_slot
    thumb_keys = lax.psum(jnp.where(mine, key_tile, jnp.zeros_like(key_tile)), "tile")
    thumb_values = lax.psum(jnp.where(mine, value_tile, jnp.zeros_like(value_tile)), "tile")
    state = (
        jnp.zeros((TOK, HH), jnp.float32),
        jnp.zeros((HEADS, TOK, 1), jnp.float32),
        jnp.zeros((HEADS, TOK, 1), jnp.float32),
    )
    arrived_last = None
    state_before = None
    for first_head, end_head in HEAD_CHUNKS:
        head_count = end_head - first_head
        cols = slice(first_head * HD, end_head * HD)
        own = jnp.concatenate([key_tile[:, cols], value_tile[:, cols]], axis=1)
        if arrived_last is not None:
            arrived_last, state_before, own = lax.optimization_barrier((arrived_last, state_before, own))
        left = passed_along(own, "tile", 1)
        right = passed_along(own, "tile", -1)
        arrived_last = (left, right)
        state_before = state
        state = attend_near(
            flags, query_tile[:, cols], (own, left, right), first_head, head_count, state
        )
    attended = attend_thumb(flags, query_tile, thumb_keys, thumb_values, *state)
    arranged = attended.reshape(device_count, per_peer, 4 * HH)
    arrived = lax.all_to_all(arranged, ("dp", "tile"), split_axis=0, concat_axis=0, tiled=True)
    own_rank = page_index * slot_count + slot_index
    sources = jnp.arange(device_count, dtype=jnp.int32)
    source_page = sources // slot_count
    source_slot = sources % slot_count
    source_grid = source_slot - firsts[source_page]
    source_thumb = source_slot == thumbs[source_page]
    source_live = (source_grid >= 0) & (source_grid < tile_totals[source_page]) | source_thumb
    source_start = (
        starts[source_page]
        + texts[source_page]
        + jnp.where(source_thumb, tile_totals[source_page], source_grid) * SHUF
    )
    first_row = (source_start + (own_rank - source_start) % device_count) // device_count
    shard_rows = SHUF + TXTMAX // slot_count
    targets = first_row[:, None] + jnp.arange(per_peer, dtype=jnp.int32)[None, :]
    targets = jnp.where(source_live[:, None], targets, shard_rows)
    placed = jnp.zeros((shard_rows, 4 * HH), jnp.bfloat16)
    return placed.at[targets.reshape(-1)].set(arrived.reshape(-1, 4 * HH), mode="drop")


def solution(mesh):
    placed = (
        P("dp", "tile", None, None),
        P("dp", "tile", None, None),
        P("dp", "tile", None, None),
        P(),
    )
    return jax.shard_map(
        body, mesh=mesh, in_specs=placed, out_specs=P(("dp", "tile"), None), check_vma=False
    )
```

```python
import jax
import jax.numpy as jnp
from jax import lax
from jax.experimental import pallas as pl
from jax.experimental.pallas import tpu as pltpu
from jax.sharding import PartitionSpec as P

HEADS = 13
HD = 128
GRID = 32
TXTMAX = 256
HH = 1664
TOK = 1024
SHUF = 256
HEAD_CHUNKS = ((0, 4), (4, 8), (8, 11), (11, 13))


def passed_along(value, axis, steps):
    count = lax.axis_size(axis)
    initial, last = (max(0, -steps), min(count, count - steps))
    return lax.ppermute(value, axis, [(source, source + steps) for source in range(initial, last)])


def block_terms(query, k_ref, v_ref):
    scores = lax.dot_general(
        query, k_ref[...], (((1,), (1,)), ((), ())), preferred_element_type=jnp.float32
    ) * HD ** (-0.5)
    largest = jnp.max(scores, axis=1, keepdims=True)
    weights = jnp.exp(scores - largest).astype(jnp.bfloat16)
    ones = jnp.ones((TOK, HD), jnp.bfloat16)
    both = jnp.dot(
        weights, jnp.concatenate([v_ref[...], ones], axis=1), preferred_element_type=jnp.float32
    )
    return both[:, :HD], largest, both[:, HD : HD + 1]


def merge_block(flag, query, k_ref, v_ref, acc_ref, top_ref, sum_ref):
    @pl.when(flag != 0)
    def _():
        numerator, largest, totals = block_terms(query, k_ref, v_ref)
        old_top = top_ref[...]
        new_top = jnp.maximum(old_top, largest)
        keep = jnp.exp(old_top - new_top)
        take = jnp.exp(largest - new_top)
        acc_ref[...] = acc_ref[...] * keep + numerator * take
        sum_ref[...] = sum_ref[...] * keep + totals * take
        top_ref[...] = new_top


def near_kernel(flags_ref, q_ref, k0, v0, k1, v1, k2, v2, acc_prev, top_prev, sum_prev, acc_ref, top_ref, sum_ref):
    query = q_ref[...]
    numerator, largest, totals = block_terms(query, k0, v0)
    acc_ref[...] = numerator
    top_ref[0] = largest
    sum_ref[0] = totals
    merge_block(flags_ref[0], query, k1, v1, acc_ref, top_ref.at[0], sum_ref.at[0])
    merge_block(flags_ref[1], query, k2, v2, acc_ref, top_ref.at[0], sum_ref.at[0])


def thumb_kernel(flags_ref, q_ref, k3, v3, acc_in, top_in, sum_in, o_ref, acc_ref, top_ref, sum_ref):
    acc_ref[...] = acc_in[...]
    top_ref[...] = top_in[0]
    sum_ref[...] = sum_in[0]
    merge_block(flags_ref[2], q_ref[...], k3, v3, acc_ref, top_ref, sum_ref)
    attended = (acc_ref[...] / sum_ref[...]).astype(o_ref.dtype)
    head = pl.program_id(0)
    for patch in range(4):
        column = pl.multiple_of(patch * HH + head * HD, HD)
        o_ref[:, pl.ds(column, HD)] = attended[patch * SHUF : (patch + 1) * SHUF]


def attend_near(flags, query_cols, blocks, first_head, head_count, state):
    q_spec = pl.BlockSpec((TOK, HD), lambda h, flags: (0, h))
    v_spec = pl.BlockSpec((TOK, HD), lambda h, flags: (0, head_count + h))
    acc_spec = pl.BlockSpec((TOK, HD), lambda h, flags: (0, first_head + h))
    stat_spec = pl.BlockSpec((1, TOK, 1), lambda h, flags: (first_head + h, 0, 0))
    held = pl.BlockSpec(memory_space=pl.ANY)
    operands = []
    for both in blocks:
        operands += [both, both]
    count = 1 + len(operands)
    return pl.pallas_call(
        near_kernel,
        grid_spec=pltpu.PrefetchScalarGridSpec(
            num_scalar_prefetch=1,
            grid=(head_count,),
            in_specs=[q_spec] + [q_spec, v_spec] * len(blocks) + [held] * 3,
            out_specs=[acc_spec, stat_spec, stat_spec],
        ),
        out_shape=[
            jax.ShapeDtypeStruct((TOK, HH), jnp.float32),
            jax.ShapeDtypeStruct((HEADS, TOK, 1), jnp.float32),
            jax.ShapeDtypeStruct((HEADS, TOK, 1), jnp.float32),
        ],
        input_output_aliases={count + 1: 0, count + 2: 1, count + 3: 2},
    )(flags, query_cols, *operands, *state)


def attend_thumb(flags, query_tile, thumb_keys, thumb_values, acc, top, totals, head_count):
    q_spec = pl.BlockSpec((TOK, HD), lambda h, flags: (0, h))
    stat_spec = pl.BlockSpec((1, TOK, 1), lambda h, flags: (h, 0, 0))
    return pl.pallas_call(
        thumb_kernel,
        grid_spec=pltpu.PrefetchScalarGridSpec(
            num_scalar_prefetch=1,
            grid=(head_count,),
            in_specs=[q_spec, q_spec, q_spec, q_spec, stat_spec, stat_spec],
            out_specs=pl.BlockSpec((SHUF, 4 * HH), lambda h, flags: (0, 0)),
            scratch_shapes=[
                pltpu.VMEM((TOK, HD), jnp.float32),
                pltpu.VMEM((TOK, 1), jnp.float32),
                pltpu.VMEM((TOK, 1), jnp.float32),
            ],
        ),
        out_shape=jax.ShapeDtypeStruct((SHUF, 4 * HH), jnp.bfloat16),
    )(flags, query_tile, thumb_keys, thumb_values, acc, top, totals)


def last_kernel(flags_ref, q_ref, k0, v0, k1, v1, k2, v2, k3, v3, out_prev, o_ref, held_ref, acc_ref, top_ref, sum_ref):
    @pl.when(pl.program_id(1) == 0)
    def _():
        query = q_ref[...]
        numerator, largest, totals = block_terms(query, k0, v0)
        acc_ref[...] = numerator
        top_ref[...] = largest
        sum_ref[...] = totals
        for index, (k_ref, v_ref) in enumerate(((k1, v1), (k2, v2), (k3, v3))):
            merge_block(flags_ref[index], query, k_ref, v_ref, acc_ref, top_ref, sum_ref)
        held_ref[...] = (acc_ref[...] / sum_ref[...]).astype(held_ref.dtype)

    patch = pl.program_id(1)
    o_ref[...] = held_ref[pl.ds(pl.multiple_of(patch * SHUF, SHUF), SHUF)]


def attend_last(flags, query_cols, blocks, thumb_keys, thumb_values, first_head, head_count, out_prev):
    q_spec = pl.BlockSpec((TOK, HD), lambda h, p, flags: (0, h))
    v_spec = pl.BlockSpec((TOK, HD), lambda h, p, flags: (0, head_count + h))
    t_spec = pl.BlockSpec((TOK, HD), lambda h, p, flags: (0, first_head + h))
    o_spec = pl.BlockSpec((SHUF, HD), lambda h, p, flags: (0, p * HEADS + first_head + h))
    operands = []
    for both in blocks:
        operands += [both, both]
    count = 1 + len(operands) + 2
    return pl.pallas_call(
        last_kernel,
        grid_spec=pltpu.PrefetchScalarGridSpec(
            num_scalar_prefetch=1,
            grid=(head_count, 4),
            in_specs=[q_spec] + [q_spec, v_spec] * len(blocks) + [t_spec, t_spec]
            + [pl.BlockSpec(memory_space=pl.ANY)],
            out_specs=o_spec,
            scratch_shapes=[
                pltpu.VMEM((TOK, HD), jnp.bfloat16),
                pltpu.VMEM((TOK, HD), jnp.float32),
                pltpu.VMEM((TOK, 1), jnp.float32),
                pltpu.VMEM((TOK, 1), jnp.float32),
            ],
        ),
        out_shape=jax.ShapeDtypeStruct((SHUF, 4 * HH), jnp.bfloat16),
        input_output_aliases={count + 1: 0},
    )(flags, query_cols, *operands, thumb_keys, thumb_values, out_prev)


def pixel_shuffle(attended):
    half_grid = GRID // 2
    width = attended.shape[-1]
    return (
        attended.reshape(half_grid, 2, half_grid, 2, width)
        .transpose(0, 2, 1, 3, 4)
        .reshape(half_grid * half_grid, 4 * width)
    )


def page_layout(page_info):
    columns = page_info[:, 0]
    tile_totals = columns * page_info[:, 1]
    thumbs = page_info[:, 2]
    texts = page_info[:, 3]
    firsts = page_info[:, 4]
    lengths = texts + (tile_totals + 1) * SHUF
    starts = jnp.cumsum(lengths) - lengths
    return (columns, tile_totals, thumbs, texts, starts, firsts)


def body(queries, keys, values, page_info):
    query_tile = queries.reshape(TOK, HH)
    key_tile = keys.reshape(TOK, HH)
    value_tile = values.reshape(TOK, HH)
    slot_count = lax.axis_size("tile")
    page_count = lax.axis_size("dp")
    device_count = page_count * slot_count
    page_index = lax.axis_index("dp")
    slot_index = lax.axis_index("tile")
    columns, tile_totals, thumbs, texts, starts, firsts = page_layout(page_info)
    grid_width = columns[page_index]
    tile_total = tile_totals[page_index]
    thumb_slot = thumbs[page_index]
    grid_pos = slot_index - firsts[page_index]
    is_tile = (grid_pos >= 0) & (grid_pos < tile_total)
    has_left = is_tile & (grid_pos % grid_width > 0)
    has_right = is_tile & (grid_pos % grid_width < grid_width - 1)
    flags = jnp.stack([has_left, has_right, is_tile]).astype(jnp.int32)
    is_thumb = slot_index == thumb_slot
    is_live = is_tile | is_thumb
    row_start = (
        starts[page_index] + texts[page_index] + jnp.where(is_thumb, tile_total, grid_pos) * SHUF
    )
    per_peer = SHUF // device_count
    query_tile = (
        jnp.roll(
            pixel_shuffle(query_tile).reshape(per_peer, device_count, 4 * HH),
            row_start % device_count,
            axis=1,
        )
        .transpose(1, 0, 2)
        .reshape(SHUF, 4, HH)
        .transpose(1, 0, 2)
        .reshape(TOK, HH)
    )

    mine = slot_index == thumb_slot
    thumb_keys = lax.psum(jnp.where(mine, key_tile, jnp.zeros_like(key_tile)), "tile")
    thumb_values = lax.psum(jnp.where(mine, value_tile, jnp.zeros_like(value_tile)), "tile")
    state = (
        jnp.zeros((TOK, HH), jnp.float32),
        jnp.zeros((HEADS, TOK, 1), jnp.float32),
        jnp.zeros((HEADS, TOK, 1), jnp.float32),
    )
    arrived_last = None
    state_before = None
    *near_chunks, (last_first, last_end) = HEAD_CHUNKS
    for first_head, end_head in near_chunks:
        head_count = end_head - first_head
        cols = slice(first_head * HD, end_head * HD)
        own = jnp.concatenate([key_tile[:, cols], value_tile[:, cols]], axis=1)
        if arrived_last is not None:
            arrived_last, state_before, own = lax.optimization_barrier((arrived_last, state_before, own))
        left = passed_along(own, "tile", 1)
        right = passed_along(own, "tile", -1)
        arrived_last = (left, right)
        state_before = state
        state = attend_near(
            flags, query_tile[:, cols], (own, left, right), first_head, head_count, state
        )
    cols = slice(last_first * HD, last_end * HD)
    own = jnp.concatenate([key_tile[:, cols], value_tile[:, cols]], axis=1)
    arrived_last, state_before, thumb_keys, thumb_values, own = lax.optimization_barrier(
        (arrived_last, state_before, thumb_keys, thumb_values, own)
    )
    left = passed_along(own, "tile", 1)
    right = passed_along(own, "tile", -1)
    attended = attend_thumb(flags, query_tile, thumb_keys, thumb_values, *state, last_first)
    attended = attend_last(
        flags,
        query_tile[:, cols],
        (own, left, right),
        thumb_keys,
        thumb_values,
        last_first,
        last_end - last_first,
        attended,
    )
    arranged = attended.reshape(device_count, per_peer, 4 * HH)
    arrived = lax.all_to_all(arranged, ("dp", "tile"), split_axis=0, concat_axis=0, tiled=True)
    own_rank = page_index * slot_count + slot_index
    sources = jnp.arange(device_count, dtype=jnp.int32)
    source_page = sources // slot_count
    source_slot = sources % slot_count
    source_grid = source_slot - firsts[source_page]
    source_thumb = source_slot == thumbs[source_page]
    source_live = (source_grid >= 0) & (source_grid < tile_totals[source_page]) | source_thumb
    source_start = (
        starts[source_page]
        + texts[source_page]
        + jnp.where(source_thumb, tile_totals[source_page], source_grid) * SHUF
    )
    first_row = (source_start + (own_rank - source_start) % device_count) // device_count
    shard_rows = SHUF + TXTMAX // slot_count
    targets = first_row[:, None] + jnp.arange(per_peer, dtype=jnp.int32)[None, :]
    targets = jnp.where(source_live[:, None], targets, shard_rows)
    placed = jnp.zeros((shard_rows, 4 * HH), jnp.bfloat16)
    return placed.at[targets.reshape(-1)].set(arrived.reshape(-1, 4 * HH), mode="drop")


def solution(mesh):
    placed = (
        P("dp", "tile", None, None),
        P("dp", "tile", None, None),
        P("dp", "tile", None, None),
        P(),
    )
    return jax.shard_map(
        body, mesh=mesh, in_specs=placed, out_specs=P(("dp", "tile"), None), check_vma=False
    )
```

```python
import jax
import jax.numpy as jnp
from jax import lax
from jax.experimental import pallas as pl
from jax.experimental.pallas import tpu as pltpu
from jax.sharding import PartitionSpec as P

HEADS = 13
HD = 128
GRID = 32
TXTMAX = 256
HH = 1664
TOK = 1024
SHUF = 256
HEAD_CHUNKS = ((0, 3), (3, 6), (6, 9), (9, 11), (11, 13))


def passed_along(value, axis, steps):
    count = lax.axis_size(axis)
    initial, last = (max(0, -steps), min(count, count - steps))
    return lax.ppermute(value, axis, [(source, source + steps) for source in range(initial, last)])


def block_terms(query, k_ref, v_ref):
    scores = lax.dot_general(
        query, k_ref[...], (((1,), (1,)), ((), ())), preferred_element_type=jnp.float32
    ) * HD ** (-0.5)
    largest = jnp.max(scores, axis=1, keepdims=True)
    weights = jnp.exp(scores - largest).astype(jnp.bfloat16)
    ones = jnp.ones((TOK, HD), jnp.bfloat16)
    both = jnp.dot(
        weights, jnp.concatenate([v_ref[...], ones], axis=1), preferred_element_type=jnp.float32
    )
    return both[:, :HD], largest, both[:, HD : HD + 1]


def merge_block(flag, query, k_ref, v_ref, acc_ref, top_ref, sum_ref):
    @pl.when(flag != 0)
    def _():
        numerator, largest, totals = block_terms(query, k_ref, v_ref)
        old_top = top_ref[...]
        new_top = jnp.maximum(old_top, largest)
        keep = jnp.exp(old_top - new_top)
        take = jnp.exp(largest - new_top)
        acc_ref[...] = acc_ref[...] * keep + numerator * take
        sum_ref[...] = sum_ref[...] * keep + totals * take
        top_ref[...] = new_top


def near_kernel(flags_ref, q_ref, k0, v0, k1, v1, k2, v2, acc_prev, top_prev, sum_prev, acc_ref, top_ref, sum_ref):
    query = q_ref[...]
    numerator, largest, totals = block_terms(query, k0, v0)
    acc_ref[...] = numerator
    top_ref[0] = largest
    sum_ref[0] = totals
    merge_block(flags_ref[0], query, k1, v1, acc_ref, top_ref.at[0], sum_ref.at[0])
    merge_block(flags_ref[1], query, k2, v2, acc_ref, top_ref.at[0], sum_ref.at[0])


def thumb_kernel(flags_ref, q_ref, k3, v3, acc_in, top_in, sum_in, o_ref, acc_ref, top_ref, sum_ref):
    acc_ref[...] = acc_in[...]
    top_ref[...] = top_in[0]
    sum_ref[...] = sum_in[0]
    merge_block(flags_ref[2], q_ref[...], k3, v3, acc_ref, top_ref, sum_ref)
    attended = (acc_ref[...] / sum_ref[...]).astype(o_ref.dtype)
    head = pl.program_id(0)
    for patch in range(4):
        column = pl.multiple_of(patch * HH + head * HD, HD)
        o_ref[:, pl.ds(column, HD)] = attended[patch * SHUF : (patch + 1) * SHUF]


def attend_near(flags, query_cols, blocks, first_head, head_count, state):
    q_spec = pl.BlockSpec((TOK, HD), lambda h, flags: (0, h))
    v_spec = pl.BlockSpec((TOK, HD), lambda h, flags: (0, head_count + h))
    acc_spec = pl.BlockSpec((TOK, HD), lambda h, flags: (0, first_head + h))
    stat_spec = pl.BlockSpec((1, TOK, 1), lambda h, flags: (first_head + h, 0, 0))
    held = pl.BlockSpec(memory_space=pl.ANY)
    operands = []
    for both in blocks:
        operands += [both, both]
    count = 1 + len(operands)
    return pl.pallas_call(
        near_kernel,
        grid_spec=pltpu.PrefetchScalarGridSpec(
            num_scalar_prefetch=1,
            grid=(head_count,),
            in_specs=[q_spec] + [q_spec, v_spec] * len(blocks) + [held] * 3,
            out_specs=[acc_spec, stat_spec, stat_spec],
        ),
        out_shape=[
            jax.ShapeDtypeStruct((TOK, HH), jnp.float32),
            jax.ShapeDtypeStruct((HEADS, TOK, 1), jnp.float32),
            jax.ShapeDtypeStruct((HEADS, TOK, 1), jnp.float32),
        ],
        input_output_aliases={count + 1: 0, count + 2: 1, count + 3: 2},
    )(flags, query_cols, *operands, *state)


def attend_thumb(flags, query_tile, thumb_keys, thumb_values, acc, top, totals):
    q_spec = pl.BlockSpec((TOK, HD), lambda h, flags: (0, h))
    stat_spec = pl.BlockSpec((1, TOK, 1), lambda h, flags: (h, 0, 0))
    return pl.pallas_call(
        thumb_kernel,
        grid_spec=pltpu.PrefetchScalarGridSpec(
            num_scalar_prefetch=1,
            grid=(HEADS,),
            in_specs=[q_spec, q_spec, q_spec, q_spec, stat_spec, stat_spec],
            out_specs=pl.BlockSpec((SHUF, 4 * HH), lambda h, flags: (0, 0)),
            scratch_shapes=[
                pltpu.VMEM((TOK, HD), jnp.float32),
                pltpu.VMEM((TOK, 1), jnp.float32),
                pltpu.VMEM((TOK, 1), jnp.float32),
            ],
        ),
        out_shape=jax.ShapeDtypeStruct((SHUF, 4 * HH), jnp.bfloat16),
    )(flags, query_tile, thumb_keys, thumb_values, acc, top, totals)


def pixel_shuffle(attended):
    half_grid = GRID // 2
    width = attended.shape[-1]
    return (
        attended.reshape(half_grid, 2, half_grid, 2, width)
        .transpose(0, 2, 1, 3, 4)
        .reshape(half_grid * half_grid, 4 * width)
    )


def page_layout(page_info):
    columns = page_info[:, 0]
    tile_totals = columns * page_info[:, 1]
    thumbs = page_info[:, 2]
    texts = page_info[:, 3]
    firsts = page_info[:, 4]
    lengths = texts + (tile_totals + 1) * SHUF
    starts = jnp.cumsum(lengths) - lengths
    return (columns, tile_totals, thumbs, texts, starts, firsts)


def body(queries, keys, values, page_info):
    query_tile = queries.reshape(TOK, HH)
    key_tile = keys.reshape(TOK, HH)
    value_tile = values.reshape(TOK, HH)
    slot_count = lax.axis_size("tile")
    page_count = lax.axis_size("dp")
    device_count = page_count * slot_count
    page_index = lax.axis_index("dp")
    slot_index = lax.axis_index("tile")
    columns, tile_totals, thumbs, texts, starts, firsts = page_layout(page_info)
    grid_width = columns[page_index]
    tile_total = tile_totals[page_index]
    thumb_slot = thumbs[page_index]
    grid_pos = slot_index - firsts[page_index]
    is_tile = (grid_pos >= 0) & (grid_pos < tile_total)
    has_left = is_tile & (grid_pos % grid_width > 0)
    has_right = is_tile & (grid_pos % grid_width < grid_width - 1)
    flags = jnp.stack([has_left, has_right, is_tile]).astype(jnp.int32)
    is_thumb = slot_index == thumb_slot
    is_live = is_tile | is_thumb
    row_start = (
        starts[page_index] + texts[page_index] + jnp.where(is_thumb, tile_total, grid_pos) * SHUF
    )
    per_peer = SHUF // device_count
    query_tile = (
        jnp.roll(
            pixel_shuffle(query_tile).reshape(per_peer, device_count, 4 * HH),
            row_start % device_count,
            axis=1,
        )
        .transpose(1, 0, 2)
        .reshape(SHUF, 4, HH)
        .transpose(1, 0, 2)
        .reshape(TOK, HH)
    )

    mine = slot_index == thumb_slot
    thumb_keys = lax.psum(jnp.where(mine, key_tile, jnp.zeros_like(key_tile)), "tile")
    thumb_values = lax.psum(jnp.where(mine, value_tile, jnp.zeros_like(value_tile)), "tile")
    state = (
        jnp.zeros((TOK, HH), jnp.float32),
        jnp.zeros((HEADS, TOK, 1), jnp.float32),
        jnp.zeros((HEADS, TOK, 1), jnp.float32),
    )
    arrived_last = None
    state_before = None
    for first_head, end_head in HEAD_CHUNKS:
        head_count = end_head - first_head
        cols = slice(first_head * HD, end_head * HD)
        own = jnp.concatenate([key_tile[:, cols], value_tile[:, cols]], axis=1)
        if arrived_last is not None:
            arrived_last, state_before, own = lax.optimization_barrier((arrived_last, state_before, own))
        left = passed_along(own, "tile", 1)
        right = passed_along(own, "tile", -1)
        arrived_last = (left, right)
        state_before = state
        state = attend_near(
            flags, query_tile[:, cols], (own, left, right), first_head, head_count, state
        )
    attended = attend_thumb(flags, query_tile, thumb_keys, thumb_values, *state)
    arranged = attended.reshape(device_count, per_peer, 4 * HH)
    arrived = lax.all_to_all(arranged, ("dp", "tile"), split_axis=0, concat_axis=0, tiled=True)
    own_rank = page_index * slot_count + slot_index
    sources = jnp.arange(device_count, dtype=jnp.int32)
    source_page = sources // slot_count
    source_slot = sources % slot_count
    source_grid = source_slot - firsts[source_page]
    source_thumb = source_slot == thumbs[source_page]
    source_live = (source_grid >= 0) & (source_grid < tile_totals[source_page]) | source_thumb
    source_start = (
        starts[source_page]
        + texts[source_page]
        + jnp.where(source_thumb, tile_totals[source_page], source_grid) * SHUF
    )
    first_row = (source_start + (own_rank - source_start) % device_count) // device_count
    shard_rows = SHUF + TXTMAX // slot_count
    targets = first_row[:, None] + jnp.arange(per_peer, dtype=jnp.int32)[None, :]
    targets = jnp.where(source_live[:, None], targets, shard_rows)
    placed = jnp.zeros((shard_rows, 4 * HH), jnp.bfloat16)
    return placed.at[targets.reshape(-1)].set(arrived.reshape(-1, 4 * HH), mode="drop")


def solution(mesh):
    placed = (
        P("dp", "tile", None, None),
        P("dp", "tile", None, None),
        P("dp", "tile", None, None),
        P(),
    )
    return jax.shard_map(
        body, mesh=mesh, in_specs=placed, out_specs=P(("dp", "tile"), None), check_vma=False
    )
```

```python
import jax
import jax.numpy as jnp
from jax import lax
from jax.experimental import pallas as pl
from jax.experimental.pallas import tpu as pltpu
from jax.sharding import PartitionSpec as P

HEADS = 13
HD = 128
GRID = 32
TXTMAX = 256
HH = 1664
TOK = 1024
SHUF = 256
HEAD_CHUNKS = ((0, 2), (2, 5), (5, 8), (8, 11), (11, 13))


def passed_along(value, axis, steps):
    count = lax.axis_size(axis)
    initial, last = (max(0, -steps), min(count, count - steps))
    return lax.ppermute(value, axis, [(source, source + steps) for source in range(initial, last)])


def block_terms(query, k_ref, v_ref):
    scores = lax.dot_general(
        query, k_ref[...], (((1,), (1,)), ((), ())), preferred_element_type=jnp.float32
    ) * HD ** (-0.5)
    largest = jnp.max(scores, axis=1, keepdims=True)
    weights = jnp.exp(scores - largest).astype(jnp.bfloat16)
    ones = jnp.ones((TOK, HD), jnp.bfloat16)
    both = jnp.dot(
        weights, jnp.concatenate([v_ref[...], ones], axis=1), preferred_element_type=jnp.float32
    )
    return both[:, :HD], largest, both[:, HD : HD + 1]


def merge_block(flag, query, k_ref, v_ref, acc_ref, top_ref, sum_ref):
    @pl.when(flag != 0)
    def _():
        numerator, largest, totals = block_terms(query, k_ref, v_ref)
        old_top = top_ref[...]
        new_top = jnp.maximum(old_top, largest)
        keep = jnp.exp(old_top - new_top)
        take = jnp.exp(largest - new_top)
        acc_ref[...] = acc_ref[...] * keep + numerator * take
        sum_ref[...] = sum_ref[...] * keep + totals * take
        top_ref[...] = new_top


def near_kernel(flags_ref, q_ref, k0, v0, k1, v1, k2, v2, acc_prev, top_prev, sum_prev, acc_ref, top_ref, sum_ref):
    query = q_ref[...]
    numerator, largest, totals = block_terms(query, k0, v0)
    acc_ref[...] = numerator
    top_ref[0] = largest
    sum_ref[0] = totals
    merge_block(flags_ref[0], query, k1, v1, acc_ref, top_ref.at[0], sum_ref.at[0])
    merge_block(flags_ref[1], query, k2, v2, acc_ref, top_ref.at[0], sum_ref.at[0])


def thumb_kernel(flags_ref, q_ref, k3, v3, acc_in, top_in, sum_in, o_ref, acc_ref, top_ref, sum_ref):
    acc_ref[...] = acc_in[...]
    top_ref[...] = top_in[0]
    sum_ref[...] = sum_in[0]
    merge_block(flags_ref[2], q_ref[...], k3, v3, acc_ref, top_ref, sum_ref)
    attended = (acc_ref[...] / sum_ref[...]).astype(o_ref.dtype)
    head = pl.program_id(0)
    for patch in range(4):
        column = pl.multiple_of(patch * HH + head * HD, HD)
        o_ref[:, pl.ds(column, HD)] = attended[patch * SHUF : (patch + 1) * SHUF]


def attend_near(flags, query_cols, blocks, first_head, head_count, state):
    q_spec = pl.BlockSpec((TOK, HD), lambda h, flags: (0, h))
    v_spec = pl.BlockSpec((TOK, HD), lambda h, flags: (0, head_count + h))
    acc_spec = pl.BlockSpec((TOK, HD), lambda h, flags: (0, first_head + h))
    stat_spec = pl.BlockSpec((1, TOK, 1), lambda h, flags: (first_head + h, 0, 0))
    held = pl.BlockSpec(memory_space=pl.ANY)
    operands = []
    for both in blocks:
        operands += [both, both]
    count = 1 + len(operands)
    return pl.pallas_call(
        near_kernel,
        grid_spec=pltpu.PrefetchScalarGridSpec(
            num_scalar_prefetch=1,
            grid=(head_count,),
            in_specs=[q_spec] + [q_spec, v_spec] * len(blocks) + [held] * 3,
            out_specs=[acc_spec, stat_spec, stat_spec],
        ),
        out_shape=[
            jax.ShapeDtypeStruct((TOK, HH), jnp.float32),
            jax.ShapeDtypeStruct((HEADS, TOK, 1), jnp.float32),
            jax.ShapeDtypeStruct((HEADS, TOK, 1), jnp.float32),
        ],
        input_output_aliases={count + 1: 0, count + 2: 1, count + 3: 2},
    )(flags, query_cols, *operands, *state)


def attend_thumb(flags, query_tile, thumb_keys, thumb_values, acc, top, totals):
    q_spec = pl.BlockSpec((TOK, HD), lambda h, flags: (0, h))
    stat_spec = pl.BlockSpec((1, TOK, 1), lambda h, flags: (h, 0, 0))
    return pl.pallas_call(
        thumb_kernel,
        grid_spec=pltpu.PrefetchScalarGridSpec(
            num_scalar_prefetch=1,
            grid=(HEADS,),
            in_specs=[q_spec, q_spec, q_spec, q_spec, stat_spec, stat_spec],
            out_specs=pl.BlockSpec((SHUF, 4 * HH), lambda h, flags: (0, 0)),
            scratch_shapes=[
                pltpu.VMEM((TOK, HD), jnp.float32),
                pltpu.VMEM((TOK, 1), jnp.float32),
                pltpu.VMEM((TOK, 1), jnp.float32),
            ],
        ),
        out_shape=jax.ShapeDtypeStruct((SHUF, 4 * HH), jnp.bfloat16),
    )(flags, query_tile, thumb_keys, thumb_values, acc, top, totals)


def pixel_shuffle(attended):
    half_grid = GRID // 2
    width = attended.shape[-1]
    return (
        attended.reshape(half_grid, 2, half_grid, 2, width)
        .transpose(0, 2, 1, 3, 4)
        .reshape(half_grid * half_grid, 4 * width)
    )


def page_layout(page_info):
    columns = page_info[:, 0]
    tile_totals = columns * page_info[:, 1]
    thumbs = page_info[:, 2]
    texts = page_info[:, 3]
    firsts = page_info[:, 4]
    lengths = texts + (tile_totals + 1) * SHUF
    starts = jnp.cumsum(lengths) - lengths
    return (columns, tile_totals, thumbs, texts, starts, firsts)


def body(queries, keys, values, page_info):
    query_tile = queries.reshape(TOK, HH)
    key_tile = keys.reshape(TOK, HH)
    value_tile = values.reshape(TOK, HH)
    slot_count = lax.axis_size("tile")
    page_count = lax.axis_size("dp")
    device_count = page_count * slot_count
    page_index = lax.axis_index("dp")
    slot_index = lax.axis_index("tile")
    columns, tile_totals, thumbs, texts, starts, firsts = page_layout(page_info)
    grid_width = columns[page_index]
    tile_total = tile_totals[page_index]
    thumb_slot = thumbs[page_index]
    grid_pos = slot_index - firsts[page_index]
    is_tile = (grid_pos >= 0) & (grid_pos < tile_total)
    has_left = is_tile & (grid_pos % grid_width > 0)
    has_right = is_tile & (grid_pos % grid_width < grid_width - 1)
    flags = jnp.stack([has_left, has_right, is_tile]).astype(jnp.int32)
    is_thumb = slot_index == thumb_slot
    is_live = is_tile | is_thumb
    row_start = (
        starts[page_index] + texts[page_index] + jnp.where(is_thumb, tile_total, grid_pos) * SHUF
    )
    per_peer = SHUF // device_count
    query_tile = (
        jnp.roll(
            pixel_shuffle(query_tile).reshape(per_peer, device_count, 4 * HH),
            row_start % device_count,
            axis=1,
        )
        .transpose(1, 0, 2)
        .reshape(SHUF, 4, HH)
        .transpose(1, 0, 2)
        .reshape(TOK, HH)
    )

    mine = slot_index == thumb_slot
    thumb_keys = lax.psum(jnp.where(mine, key_tile, jnp.zeros_like(key_tile)), "tile")
    thumb_values = lax.psum(jnp.where(mine, value_tile, jnp.zeros_like(value_tile)), "tile")
    state = (
        jnp.zeros((TOK, HH), jnp.float32),
        jnp.zeros((HEADS, TOK, 1), jnp.float32),
        jnp.zeros((HEADS, TOK, 1), jnp.float32),
    )
    arrived_last = None
    state_before = None
    for first_head, end_head in HEAD_CHUNKS:
        head_count = end_head - first_head
        cols = slice(first_head * HD, end_head * HD)
        own = jnp.concatenate([key_tile[:, cols], value_tile[:, cols]], axis=1)
        if arrived_last is not None:
            arrived_last, state_before, own = lax.optimization_barrier((arrived_last, state_before, own))
        left = passed_along(own, "tile", 1)
        right = passed_along(own, "tile", -1)
        arrived_last = (left, right)
        state_before = state
        state = attend_near(
            flags, query_tile[:, cols], (own, left, right), first_head, head_count, state
        )
    attended = attend_thumb(flags, query_tile, thumb_keys, thumb_values, *state)
    arranged = attended.reshape(device_count, per_peer, 4 * HH)
    arrived = lax.all_to_all(arranged, ("dp", "tile"), split_axis=0, concat_axis=0, tiled=True)
    own_rank = page_index * slot_count + slot_index
    sources = jnp.arange(device_count, dtype=jnp.int32)
    source_page = sources // slot_count
    source_slot = sources % slot_count
    source_grid = source_slot - firsts[source_page]
    source_thumb = source_slot == thumbs[source_page]
    source_live = (source_grid >= 0) & (source_grid < tile_totals[source_page]) | source_thumb
    source_start = (
        starts[source_page]
        + texts[source_page]
        + jnp.where(source_thumb, tile_totals[source_page], source_grid) * SHUF
    )
    first_row = (source_start + (own_rank - source_start) % device_count) // device_count
    shard_rows = SHUF + TXTMAX // slot_count
    targets = first_row[:, None] + jnp.arange(per_peer, dtype=jnp.int32)[None, :]
    targets = jnp.where(source_live[:, None], targets, shard_rows)
    placed = jnp.zeros((shard_rows, 4 * HH), jnp.bfloat16)
    return placed.at[targets.reshape(-1)].set(arrived.reshape(-1, 4 * HH), mode="drop")


def solution(mesh):
    placed = (
        P("dp", "tile", None, None),
        P("dp", "tile", None, None),
        P("dp", "tile", None, None),
        P(),
    )
    return jax.shard_map(
        body, mesh=mesh, in_specs=placed, out_specs=P(("dp", "tile"), None), check_vma=False
    )
```

```python
import jax
import jax.numpy as jnp
from jax import lax
from jax.experimental import pallas as pl
from jax.experimental.pallas import tpu as pltpu
from jax.sharding import PartitionSpec as P

HEADS = 13
HD = 128
GRID = 32
TXTMAX = 256
HH = 1664
TOK = 1024
SHUF = 256
HEAD_CHUNKS = ((0, 3), (3, 6), (6, 9), (9, 12), (12, 13))


def passed_along(value, axis, steps):
    count = lax.axis_size(axis)
    initial, last = (max(0, -steps), min(count, count - steps))
    return lax.ppermute(value, axis, [(source, source + steps) for source in range(initial, last)])


def block_terms(query, k_ref, v_ref):
    scores = lax.dot_general(
        query, k_ref[...], (((1,), (1,)), ((), ())), preferred_element_type=jnp.float32
    ) * HD ** (-0.5)
    largest = jnp.max(scores, axis=1, keepdims=True)
    weights = jnp.exp(scores - largest).astype(jnp.bfloat16)
    ones = jnp.ones((TOK, HD), jnp.bfloat16)
    both = jnp.dot(
        weights, jnp.concatenate([v_ref[...], ones], axis=1), preferred_element_type=jnp.float32
    )
    return both[:, :HD], largest, both[:, HD : HD + 1]


def merge_block(flag, query, k_ref, v_ref, acc_ref, top_ref, sum_ref):
    @pl.when(flag != 0)
    def _():
        numerator, largest, totals = block_terms(query, k_ref, v_ref)
        old_top = top_ref[...]
        new_top = jnp.maximum(old_top, largest)
        keep = jnp.exp(old_top - new_top)
        take = jnp.exp(largest - new_top)
        acc_ref[...] = acc_ref[...] * keep + numerator * take
        sum_ref[...] = sum_ref[...] * keep + totals * take
        top_ref[...] = new_top


def near_kernel(flags_ref, q_ref, k0, v0, k1, v1, k2, v2, acc_prev, top_prev, sum_prev, acc_ref, top_ref, sum_ref):
    query = q_ref[...]
    numerator, largest, totals = block_terms(query, k0, v0)
    acc_ref[...] = numerator
    top_ref[0] = largest
    sum_ref[0] = totals
    merge_block(flags_ref[0], query, k1, v1, acc_ref, top_ref.at[0], sum_ref.at[0])
    merge_block(flags_ref[1], query, k2, v2, acc_ref, top_ref.at[0], sum_ref.at[0])


def thumb_kernel(flags_ref, q_ref, k3, v3, acc_in, top_in, sum_in, o_ref, acc_ref, top_ref, sum_ref):
    acc_ref[...] = acc_in[...]
    top_ref[...] = top_in[0]
    sum_ref[...] = sum_in[0]
    merge_block(flags_ref[2], q_ref[...], k3, v3, acc_ref, top_ref, sum_ref)
    attended = (acc_ref[...] / sum_ref[...]).astype(o_ref.dtype)
    head = pl.program_id(0)
    for patch in range(4):
        column = pl.multiple_of(patch * HH + head * HD, HD)
        o_ref[:, pl.ds(column, HD)] = attended[patch * SHUF : (patch + 1) * SHUF]


def attend_near(flags, query_cols, blocks, first_head, head_count, state):
    q_spec = pl.BlockSpec((TOK, HD), lambda h, flags: (0, h))
    v_spec = pl.BlockSpec((TOK, HD), lambda h, flags: (0, head_count + h))
    acc_spec = pl.BlockSpec((TOK, HD), lambda h, flags: (0, first_head + h))
    stat_spec = pl.BlockSpec((1, TOK, 1), lambda h, flags: (first_head + h, 0, 0))
    held = pl.BlockSpec(memory_space=pl.ANY)
    operands = []
    for both in blocks:
        operands += [both, both]
    count = 1 + len(operands)
    return pl.pallas_call(
        near_kernel,
        grid_spec=pltpu.PrefetchScalarGridSpec(
            num_scalar_prefetch=1,
            grid=(head_count,),
            in_specs=[q_spec] + [q_spec, v_spec] * len(blocks) + [held] * 3,
            out_specs=[acc_spec, stat_spec, stat_spec],
        ),
        out_shape=[
            jax.ShapeDtypeStruct((TOK, HH), jnp.float32),
            jax.ShapeDtypeStruct((HEADS, TOK, 1), jnp.float32),
            jax.ShapeDtypeStruct((HEADS, TOK, 1), jnp.float32),
        ],
        input_output_aliases={count + 1: 0, count + 2: 1, count + 3: 2},
    )(flags, query_cols, *operands, *state)


def attend_thumb(flags, query_tile, thumb_keys, thumb_values, acc, top, totals):
    q_spec = pl.BlockSpec((TOK, HD), lambda h, flags: (0, h))
    stat_spec = pl.BlockSpec((1, TOK, 1), lambda h, flags: (h, 0, 0))
    return pl.pallas_call(
        thumb_kernel,
        grid_spec=pltpu.PrefetchScalarGridSpec(
            num_scalar_prefetch=1,
            grid=(HEADS,),
            in_specs=[q_spec, q_spec, q_spec, q_spec, stat_spec, stat_spec],
            out_specs=pl.BlockSpec((SHUF, 4 * HH), lambda h, flags: (0, 0)),
            scratch_shapes=[
                pltpu.VMEM((TOK, HD), jnp.float32),
                pltpu.VMEM((TOK, 1), jnp.float32),
                pltpu.VMEM((TOK, 1), jnp.float32),
            ],
        ),
        out_shape=jax.ShapeDtypeStruct((SHUF, 4 * HH), jnp.bfloat16),
    )(flags, query_tile, thumb_keys, thumb_values, acc, top, totals)


def pixel_shuffle(attended):
    half_grid = GRID // 2
    width = attended.shape[-1]
    return (
        attended.reshape(half_grid, 2, half_grid, 2, width)
        .transpose(0, 2, 1, 3, 4)
        .reshape(half_grid * half_grid, 4 * width)
    )


def page_layout(page_info):
    columns = page_info[:, 0]
    tile_totals = columns * page_info[:, 1]
    thumbs = page_info[:, 2]
    texts = page_info[:, 3]
    firsts = page_info[:, 4]
    lengths = texts + (tile_totals + 1) * SHUF
    starts = jnp.cumsum(lengths) - lengths
    return (columns, tile_totals, thumbs, texts, starts, firsts)


def body(queries, keys, values, page_info):
    query_tile = queries.reshape(TOK, HH)
    key_tile = keys.reshape(TOK, HH)
    value_tile = values.reshape(TOK, HH)
    slot_count = lax.axis_size("tile")
    page_count = lax.axis_size("dp")
    device_count = page_count * slot_count
    page_index = lax.axis_index("dp")
    slot_index = lax.axis_index("tile")
    columns, tile_totals, thumbs, texts, starts, firsts = page_layout(page_info)
    grid_width = columns[page_index]
    tile_total = tile_totals[page_index]
    thumb_slot = thumbs[page_index]
    grid_pos = slot_index - firsts[page_index]
    is_tile = (grid_pos >= 0) & (grid_pos < tile_total)
    has_left = is_tile & (grid_pos % grid_width > 0)
    has_right = is_tile & (grid_pos % grid_width < grid_width - 1)
    flags = jnp.stack([has_left, has_right, is_tile]).astype(jnp.int32)
    is_thumb = slot_index == thumb_slot
    is_live = is_tile | is_thumb
    row_start = (
        starts[page_index] + texts[page_index] + jnp.where(is_thumb, tile_total, grid_pos) * SHUF
    )
    per_peer = SHUF // device_count
    query_tile = (
        jnp.roll(
            pixel_shuffle(query_tile).reshape(per_peer, device_count, 4 * HH),
            row_start % device_count,
            axis=1,
        )
        .transpose(1, 0, 2)
        .reshape(SHUF, 4, HH)
        .transpose(1, 0, 2)
        .reshape(TOK, HH)
    )

    mine = slot_index == thumb_slot
    thumb_keys = lax.psum(jnp.where(mine, key_tile, jnp.zeros_like(key_tile)), "tile")
    thumb_values = lax.psum(jnp.where(mine, value_tile, jnp.zeros_like(value_tile)), "tile")
    state = (
        jnp.zeros((TOK, HH), jnp.float32),
        jnp.zeros((HEADS, TOK, 1), jnp.float32),
        jnp.zeros((HEADS, TOK, 1), jnp.float32),
    )
    arrived_last = None
    state_before = None
    for first_head, end_head in HEAD_CHUNKS:
        head_count = end_head - first_head
        cols = slice(first_head * HD, end_head * HD)
        own = jnp.concatenate([key_tile[:, cols], value_tile[:, cols]], axis=1)
        if arrived_last is not None:
            arrived_last, state_before, own = lax.optimization_barrier((arrived_last, state_before, own))
        left = passed_along(own, "tile", 1)
        right = passed_along(own, "tile", -1)
        arrived_last = (left, right)
        state_before = state
        state = attend_near(
            flags, query_tile[:, cols], (own, left, right), first_head, head_count, state
        )
    attended = attend_thumb(flags, query_tile, thumb_keys, thumb_values, *state)
    arranged = attended.reshape(device_count, per_peer, 4 * HH)
    arrived = lax.all_to_all(arranged, ("dp", "tile"), split_axis=0, concat_axis=0, tiled=True)
    own_rank = page_index * slot_count + slot_index
    sources = jnp.arange(device_count, dtype=jnp.int32)
    source_page = sources // slot_count
    source_slot = sources % slot_count
    source_grid = source_slot - firsts[source_page]
    source_thumb = source_slot == thumbs[source_page]
    source_live = (source_grid >= 0) & (source_grid < tile_totals[source_page]) | source_thumb
    source_start = (
        starts[source_page]
        + texts[source_page]
        + jnp.where(source_thumb, tile_totals[source_page], source_grid) * SHUF
    )
    first_row = (source_start + (own_rank - source_start) % device_count) // device_count
    shard_rows = SHUF + TXTMAX // slot_count
    targets = first_row[:, None] + jnp.arange(per_peer, dtype=jnp.int32)[None, :]
    targets = jnp.where(source_live[:, None], targets, shard_rows)
    placed = jnp.zeros((shard_rows, 4 * HH), jnp.bfloat16)
    return placed.at[targets.reshape(-1)].set(arrived.reshape(-1, 4 * HH), mode="drop")


def solution(mesh):
    placed = (
        P("dp", "tile", None, None),
        P("dp", "tile", None, None),
        P("dp", "tile", None, None),
        P(),
    )
    return jax.shard_map(
        body, mesh=mesh, in_specs=placed, out_specs=P(("dp", "tile"), None), check_vma=False
    )
```
